32 devices in a mesh: cfg: 2 (over core), row: 4 (over z), col: 4 (over y, x).
Axes of the slice: x: 2, y: 2, z: 4, core: 2. Of those that a mesh axis runs over, the one named last changes fastest.
Arguments:
- image_tokens: bfloat16 [2, 3, 1024, 2432], P('cfg', None, ('row', 'col')), may hold values from -6 to 6
- text_tokens: bfloat16 [2, 3, 160, 2432], P('cfg', None, 'row'), may hold values from -6 to 6
- text_lengths: int32 [2, 3], P('cfg'), may hold values from 1 to 160, as said below
- modulation: float32 [2, 3, 10, 2432], P('cfg'), may hold values from -4 to 4
- qk_gains: float32 [3, 64], replicated, may hold values from 1 to 3
- qkv_weight: bfloat16 [2432, 32, 192], P(None, 'row'), may hold values from -0.125 to 0.125
- text_kv_weight: bfloat16 [2432, 32, 128], P(None, 'row'), may hold values from -0.125 to 0.125
- out_weight: bfloat16 [32, 64, 2432], P('row'), may hold values from -0.125 to 0.125
- up_weight: bfloat16 [2432, 9728], P(None, 'row'), may hold values from -0.125 to 0.125
- down_weight: bfloat16 [9728, 2432], P('row'), may hold values from -0.0625 to 0.0625
- final_weight: bfloat16 [2432, 64], replicated, may hold values from -0.125 to 0.125
- latents: float32 [3, 1024, 64], P(None, ('row', 'col'), 'cfg'), may hold values from -6 to 6
- sigmas: float32 [29], replicated, may hold values from 0 to 1
- step_index: int32 [1], replicated, may hold values from 0 to 27
- guidance: float32 [1], replicated, may hold values from 2 to 5
Outputs:
- velocity: float32 [3, 1024, 64], P(None, ('row', 'col'), 'cfg')
- next_latents: float32 [3, 1024, 64], P(None, ('row', 'col'), 'cfg')
The draws below stay inside these ranges and needn't reach their ends.
Inputs may be any that keep to these rules, and one draw needn't show every extreme that they name: `text_lengths`: text tokens of a prompt at positions below its length are valid. In every draw some prompt of some half has all 160.
All inputs are finite; a program needn't handle non-finite values.
Results may differ from the reference program's by a relative error of at most 0.02.
Values may be sent and summed in bfloat16 or wider, within the bound.
No kernel may reach another device: no remote copies, remote signals or barrier semaphores. Data moves between devices by JAX's collectives and lax.ppermute only.
A program may use at most 128 MiB of HBM per device.

```python
import math
import jax
import jax.numpy as jnp
from jax import lax

D = 2432
HEADS = 32
HEAD = 64
FF = 9728
PATCH = 64
IMG = 1024
TXT = 160
PROMPTS = 3
STEPS = 28


def draw_text_lengths(key, part):
    base = jax.random.randint(jax.random.fold_in(key, 11), (2 * PROMPTS,), 1, TXT + 1)
    spot = jax.random.randint(jax.random.fold_in(key, 12), (), 0, 2 * PROMPTS)
    places = jnp.arange(2 * PROMPTS)
    filled = jnp.where(places == spot, TXT, base)
    return filled.reshape(2, PROMPTS).astype(jnp.int32)


def shard_levels(own_key, extent, shards, low, largest):
    loudness, own = 1.0, jax.random.fold_in(own_key, 6)
    for axis_at, blocks in shards:
        steps = jnp.exp(jax.random.uniform(jax.random.fold_in(own, axis_at), (blocks,), jnp.float32, low / len(shards), largest / len(shards)))
        loudness = loudness * jnp.repeat(steps, extent[axis_at] // blocks).reshape([-1 if axis == axis_at else 1 for axis in range(len(extent))])
    return loudness


def scatter_about(rng, dims, width, reach, pieces=(), kind=jnp.bfloat16):
    result = width * jax.random.normal(rng, dims, jnp.float32)
    if pieces:
        result = result * shard_levels(rng, dims, pieces, -0.22, 0.18)
    return jnp.clip(result, -reach, reach).astype(kind)


def setup_inputs(seed: int = 0) -> dict:
    key_list = jax.random.split(jax.random.key(seed), 16)
    image_tokens = scatter_about(key_list[0], (2, PROMPTS, IMG, D), 1.0, 6.0, ((0, 2), (2, 16)))
    text_tokens = scatter_about(key_list[1], (2, PROMPTS, TXT, D), 1.0, 6.0, ((0, 2), (2, 4)))
    text_lengths = draw_text_lengths(jax.random.fold_in(key_list[15], 71), 0)
    modulation = scatter_about(key_list[3], (2, PROMPTS, 10, D), 1.0, 4.0, ((0, 2),), jnp.float32)
    qk_gains = jnp.clip(jnp.exp(jax.random.uniform(key_list[4], (3, HEAD), jnp.float32, math.log(1.0), math.log(3.0))), 1.0, 3.0)
    qkv_weight = scatter_about(key_list[5], (D, HEADS, 3 * HEAD), D ** -0.5, 0.125, ((1, 4),))
    text_kv_weight = scatter_about(key_list[6], (D, HEADS, 2 * HEAD), D ** -0.5, 0.125, ((1, 4),))
    out_weight = scatter_about(key_list[7], (HEADS, HEAD, D), (HEADS * HEAD) ** -0.5, 0.125, ((0, 4),))
    up_weight = scatter_about(key_list[8], (D, FF), D ** -0.5, 0.125, ((1, 4),))
    down_weight = scatter_about(key_list[9], (FF, D), FF ** -0.5, 0.0625, ((0, 4),))
    final_weight = scatter_about(key_list[10], (D, PATCH), D ** -0.5, 0.125)
    latents = scatter_about(key_list[11], (PROMPTS, IMG, PATCH), 1.0, 6.0, ((1, 16), (2, 2)), jnp.float32)
    sigmas = jnp.clip(jax.random.uniform(key_list[12], (STEPS + 1,), jnp.float32, 0.0, 1.0), 0.0, 1.0)
    step_index = jax.random.randint(key_list[13], (1,), 0, STEPS).astype(jnp.int32)
    guidance = jnp.clip(jax.random.uniform(key_list[14], (1,), jnp.float32, 2.0, 5.0), 2.0, 5.0)
    return {"image_tokens": image_tokens, "text_tokens": text_tokens, "text_lengths": text_lengths, "modulation": modulation, "qk_gains": qk_gains, "qkv_weight": qkv_weight, "text_kv_weight": text_kv_weight, "out_weight": out_weight, "up_weight": up_weight, "down_weight": down_weight, "final_weight": final_weight, "latents": latents, "sigmas": sigmas, "step_index": step_index, "guidance": guidance}


epsilon = 1e-06

def layer_norm(inputs):
    average = lax.optimization_barrier(jnp.mean(inputs, axis=-1, keepdims=True))
    centered = inputs - average
    variance = lax.optimization_barrier(jnp.mean(centered * centered, axis=-1, keepdims=True))
    return centered / jnp.sqrt(variance + epsilon)

def modulate(inputs, shifts, scales):
    return layer_norm(inputs) * (1.0 + scales) + shifts

def rms_norm(inputs, norm_gain):
    square_mean = lax.optimization_barrier(jnp.mean(inputs * inputs, axis=-1, keepdims=True))
    return inputs / jnp.sqrt(square_mean + epsilon) * norm_gain

def reference(image_tokens, text_tokens, text_lengths, modulation, qk_gains, qkv_weight, text_kv_weight, out_weight, up_weight, down_weight, final_weight, latents, sigmas, step_index, guidance):
    modifiers = modulation[:, :, :, None, :]
    image_float = image_tokens.astype(jnp.float32)
    image_in = modulate(image_float, modifiers[:, :, 0], modifiers[:, :, 1]).astype(jnp.bfloat16)
    text_in = modulate(text_tokens.astype(jnp.float32), modifiers[:, :, 6], modifiers[:, :, 7]).astype(jnp.bfloat16)
    projected = jnp.dot(image_in.reshape(-1, D), qkv_weight.reshape(D, -1), preferred_element_type=jnp.float32)
    projected = projected.reshape(2, PROMPTS, IMG, HEADS, 3 * HEAD)
    queries = rms_norm(projected[..., :HEAD], qk_gains[0]).astype(jnp.bfloat16)
    image_key = rms_norm(projected[..., HEAD:2 * HEAD], qk_gains[1]).astype(jnp.bfloat16)
    image_value = projected[..., 2 * HEAD:].astype(jnp.bfloat16)
    text_proj = jnp.dot(text_in.reshape(-1, D), text_kv_weight.reshape(D, -1), preferred_element_type=jnp.float32)
    text_proj = text_proj.reshape(2, PROMPTS, TXT, HEADS, 2 * HEAD)
    text_key = rms_norm(text_proj[..., :HEAD], qk_gains[2]).astype(jnp.bfloat16)
    text_value = text_proj[..., HEAD:].astype(jnp.bfloat16)
    keys_all = jnp.concatenate([image_key, text_key], axis=2)
    values_all = jnp.concatenate([image_value, text_value], axis=2)
    positions = jnp.arange(IMG + TXT)
    valid_keys = ((positions[None, None, :] < IMG) | (positions[None, None, :] - IMG < text_lengths[:, :, None])).astype(jnp.float32)

    def one_head(operands):
        head_queries, head_keys, head_values = operands
        scores = jnp.einsum('cpqd,cpkd->cpqk', head_queries.astype(jnp.float32), head_keys.astype(jnp.float32)) * HEAD ** (-0.5)
        weights = jnp.exp(scores) * valid_keys[:, :, None, :]
        denominator = lax.optimization_barrier(jnp.sum(weights, axis=-1, keepdims=True))
        shares = (weights / denominator).astype(jnp.bfloat16)
        return jnp.einsum('cpqk,cpkd->cpqd', shares.astype(jnp.float32), head_values.astype(jnp.float32)).astype(jnp.bfloat16)
    head_out = lax.map(one_head, (jnp.moveaxis(queries, 3, 0), jnp.moveaxis(keys_all, 3, 0), jnp.moveaxis(values_all, 3, 0)))
    head_out = jnp.moveaxis(head_out, 0, 3).reshape(-1, HEADS * HEAD)
    attention = jnp.dot(head_out, out_weight.reshape(HEADS * HEAD, D), preferred_element_type=jnp.float32)
    attention = attention.reshape(2, PROMPTS, IMG, D)
    mid_rows = image_float + modifiers[:, :, 2] * attention
    normed = modulate(mid_rows, modifiers[:, :, 3], modifiers[:, :, 4]).astype(jnp.bfloat16)
    hidden_units = jax.nn.gelu(jnp.dot(normed.reshape(-1, D), up_weight, preferred_element_type=jnp.float32), approximate=True).astype(jnp.bfloat16)
    feed = jnp.dot(hidden_units, down_weight, preferred_element_type=jnp.float32).reshape(2, PROMPTS, IMG, D)
    final_rows = mid_rows + modifiers[:, :, 5] * feed
    final_in = modulate(final_rows, modifiers[:, :, 8], modifiers[:, :, 9]).astype(jnp.bfloat16)
    half_velocity = jnp.dot(final_in.reshape(-1, D), final_weight, preferred_element_type=jnp.float32)
    half_velocity = half_velocity.reshape(2, PROMPTS, IMG, PATCH)
    velocity = half_velocity[1] + guidance[0] * (half_velocity[0] - half_velocity[1])
    sigma_pair = lax.dynamic_slice_in_dim(sigmas, step_index[0], 2, 0)
    return (velocity, latents + (sigma_pair[1] - sigma_pair[0]) * velocity)
```

```python
import jax
import jax.numpy as jnp
from jax import lax
from jax.sharding import PartitionSpec as P

HEAD = 64


epsilon = 1e-06


def layer_norm(inputs):
    average = jnp.mean(inputs, axis=-1, keepdims=True)
    centered = inputs - average
    variance = jnp.mean(centered * centered, axis=-1, keepdims=True)
    return centered / jnp.sqrt(variance + epsilon)


def modulate(inputs, shifts, scales):
    return layer_norm(inputs) * (1.0 + scales) + shifts


def rms_norm(inputs, norm_gain):
    square_mean = jnp.mean(inputs * inputs, axis=-1, keepdims=True)
    return inputs / jnp.sqrt(square_mean + epsilon) * norm_gain


def gather_any_order(x, name):
    n = lax.axis_size(name)
    m = 1
    while m < n:
        pairs = [(i, i ^ m) for i in range(n)]
        x = jnp.concatenate([x, lax.ppermute(x, name, pairs)], axis=0)
        m *= 2
    return x


def shards(
    image_tokens,
    text_tokens,
    text_lengths,
    modulation,
    qk_gains,
    qkv_weight,
    text_kv_weight,
    out_weight,
    up_weight,
    down_weight,
    final_weight,
    latents,
    sigmas,
    step_index,
    guidance,
):
    modifiers = modulation[0]
    prompts = image_tokens.shape[1]
    own_rows = image_tokens.shape[2]
    model_width = image_tokens.shape[3]
    rows_n = lax.axis_size("row")
    cols_n = lax.axis_size("col")
    local_heads = qkv_weight.shape[1]
    score_scale = HEAD ** (-0.5)

    text_own = jnp.transpose(text_tokens[0], (1, 0, 2)).astype(jnp.float32)
    text_in = modulate(text_own, modifiers[:, 6], modifiers[:, 7]).astype(jnp.bfloat16)
    text_local = text_in.shape[0]
    row_idx = lax.axis_index("row")
    col_idx = lax.axis_index("col")
    if text_local % cols_n == 0 and cols_n & (cols_n - 1) == 0:
        sub = text_local // cols_n
        piece = lax.dynamic_slice_in_dim(text_in, col_idx * sub, sub, 0)
        piece = lax.all_gather(piece, "row", axis=0, tiled=True)
        text_rows = gather_any_order(piece, "col")
        src_col = jnp.bitwise_xor(col_idx, jnp.arange(cols_n))
        positions = (
            src_col[:, None, None] * sub
            + jnp.arange(rows_n)[None, :, None] * text_local
            + jnp.arange(sub)[None, None, :]
        ).reshape(-1)
    else:
        text_rows = lax.all_gather(text_in, "row", axis=0, tiled=True)
        positions = jnp.arange(text_rows.shape[0])
    text_count = text_rows.shape[0]
    text_proj = jnp.dot(
        text_rows.reshape(-1, model_width),
        text_kv_weight.reshape(model_width, -1),
        preferred_element_type=jnp.float32,
    )
    text_proj = text_proj.reshape(text_count, prompts, local_heads, 2 * HEAD)
    text_key = rms_norm(text_proj[..., :HEAD], qk_gains[2]).astype(jnp.bfloat16)
    text_value = text_proj[..., HEAD:].astype(jnp.bfloat16)
    text_valid = (positions[None, :] < text_lengths[0][:, None]).astype(jnp.float32)

    qkv_flat = qkv_weight.reshape(model_width, -1)
    out_flat = out_weight.reshape(local_heads * HEAD, model_width)
    velocities = []
    for p in range(prompts):
        mods = modifiers[p]
        image_rows = lax.all_gather(image_tokens[0, p], "row", axis=0, tiled=True)
        query_count = image_rows.shape[0]
        image_float = image_rows.astype(jnp.float32)
        image_in = modulate(image_float, mods[0], mods[1]).astype(jnp.bfloat16)
        projected = jnp.dot(image_in, qkv_flat, preferred_element_type=jnp.float32)
        projected = projected.reshape(query_count, local_heads, 3 * HEAD)
        queries = rms_norm(projected[..., :HEAD], qk_gains[0]).astype(jnp.bfloat16)
        image_key = rms_norm(projected[..., HEAD : 2 * HEAD], qk_gains[1]).astype(jnp.bfloat16)
        image_value = projected[..., 2 * HEAD :].astype(jnp.bfloat16)
        key_value = jnp.concatenate([image_key, image_value], axis=-1)
        all_pairs = gather_any_order(key_value, "col")
        image_weights = jnp.exp(
            jnp.einsum(
                "qhd,khd->hqk", queries, all_pairs[..., :HEAD], preferred_element_type=jnp.float32
            )
            * score_scale
        )
        text_weights = jnp.exp(
            jnp.einsum("qhd,khd->hqk", queries, text_key[:, p], preferred_element_type=jnp.float32)
            * score_scale
        )
        text_weights = text_weights * text_valid[p][None, None, :]
        denominator = jnp.sum(image_weights, axis=-1, keepdims=True) + jnp.sum(
            text_weights, axis=-1, keepdims=True
        )
        image_shares = (image_weights / denominator).astype(jnp.bfloat16)
        text_shares = (text_weights / denominator).astype(jnp.bfloat16)
        mixed = jnp.einsum(
            "hqk,khd->qhd", image_shares, all_pairs[..., HEAD:], preferred_element_type=jnp.float32
        )
        mixed = mixed + jnp.einsum(
            "hqk,khd->qhd", text_shares, text_value[:, p], preferred_element_type=jnp.float32
        )
        head_rows = mixed.astype(jnp.bfloat16).reshape(query_count, local_heads * HEAD)
        partial_value = jnp.dot(head_rows, out_flat, preferred_element_type=jnp.float32)
        attention = lax.psum_scatter(
            partial_value.astype(jnp.bfloat16), "row", scatter_dimension=0, tiled=True
        ).astype(jnp.float32)
        mid_own = image_tokens[0, p].astype(jnp.float32) + mods[2] * attention
        normed_own = modulate(mid_own, mods[3], mods[4]).astype(jnp.bfloat16)
        normed = lax.all_gather(normed_own, "row", axis=0, tiled=True)
        hidden_units = jax.nn.gelu(
            jnp.dot(normed, up_weight, preferred_element_type=jnp.float32),
            approximate=True,
        ).astype(jnp.bfloat16)
        product = jnp.dot(hidden_units, down_weight, preferred_element_type=jnp.float32)
        feed = lax.psum_scatter(
            product.astype(jnp.bfloat16), "row", scatter_dimension=0, tiled=True
        ).astype(jnp.float32)
        final_rows = mid_own + mods[5] * feed
        final_in = modulate(final_rows, mods[8], mods[9]).astype(jnp.bfloat16)
        velocities.append(jnp.dot(final_in, final_weight, preferred_element_type=jnp.float32))
    own_velocity = jnp.stack(velocities, axis=1)
    own_velocity = own_velocity.reshape(1, own_rows, prompts, -1)
    both_halves = lax.all_to_all(own_velocity, "cfg", split_axis=3, concat_axis=0, tiled=True)
    conditional = both_halves[0]
    unconditional = both_halves[1]
    guided = unconditional + guidance[0] * (conditional - unconditional)
    velocity = jnp.transpose(guided, (1, 0, 2))
    sigma_pair = lax.dynamic_slice_in_dim(sigmas, step_index[0], 2, 0)
    return (velocity, latents + (sigma_pair[1] - sigma_pair[0]) * velocity)


def solution(mesh):
    placed = (
        P("cfg", None, ("row", "col"), None),
        P("cfg", None, "row", None),
        P("cfg", None),
        P("cfg", None, None, None),
        P(),
        P(None, "row", None),
        P(None, "row", None),
        P("row", None, None),
        P(None, "row"),
        P("row", None),
        P(),
        P(None, ("row", "col"), "cfg"),
        P(),
        P(),
        P(),
    )
    return jax.shard_map(
        shards,
        mesh=mesh,
        in_specs=placed,
        out_specs=(P(None, ("row", "col"), "cfg"), P(None, ("row", "col"), "cfg")),
        check_vma=False,
    )
```

```python
import jax
import jax.numpy as jnp
from jax import lax
from jax.sharding import PartitionSpec as P

HEAD = 64


epsilon = 1e-06


def layer_norm(inputs):
    average = jnp.mean(inputs, axis=-1, keepdims=True)
    centered = inputs - average
    variance = jnp.mean(centered * centered, axis=-1, keepdims=True)
    return centered / jnp.sqrt(variance + epsilon)


def modulate(inputs, shifts, scales):
    return layer_norm(inputs) * (1.0 + scales) + shifts


def rms_norm(inputs, norm_gain):
    square_mean = jnp.mean(inputs * inputs, axis=-1, keepdims=True)
    return inputs / jnp.sqrt(square_mean + epsilon) * norm_gain


def gather_any_order(x, name):
    n = lax.axis_size(name)
    m = 1
    while m < n:
        pairs = [(i, i ^ m) for i in range(n)]
        x = jnp.concatenate([x, lax.ppermute(x, name, pairs)], axis=0)
        m *= 2
    return x


def reduce_scatter_line(x, name):
    n = lax.axis_size(name)
    if n > 4:
        return lax.psum_scatter(x, name, scatter_dimension=0, tiled=True).astype(jnp.float32)
    me = lax.axis_index(name)
    size = x.shape[0] // n
    blocks = x.reshape(n, size, *x.shape[1:])

    def block(index):
        return lax.dynamic_index_in_dim(blocks, jnp.clip(index, 0, n - 1), 0, keepdims=False)

    own = block(me).astype(jnp.float32)
    up = None
    down = None
    for s in range(1, n):
        up_buf = block(me + n - s).astype(jnp.float32)
        down_buf = block(me - n + s).astype(jnp.float32)
        if up is not None:
            up_buf = up_buf + up
            down_buf = down_buf + down
        up = lax.ppermute(
            up_buf.astype(x.dtype), name, [(k, k + 1) for k in range(s)]
        ).astype(jnp.float32)
        down = lax.ppermute(
            down_buf.astype(x.dtype), name, [(k, k - 1) for k in range(n - s, n)]
        ).astype(jnp.float32)
    if up is None:
        return own
    return own + up + down


def shards(
    image_tokens,
    text_tokens,
    text_lengths,
    modulation,
    qk_gains,
    qkv_weight,
    text_kv_weight,
    out_weight,
    up_weight,
    down_weight,
    final_weight,
    latents,
    sigmas,
    step_index,
    guidance,
):
    modifiers = modulation[0]
    prompts = image_tokens.shape[1]
    own_rows = image_tokens.shape[2]
    model_width = image_tokens.shape[3]
    rows_n = lax.axis_size("row")
    cols_n = lax.axis_size("col")
    local_heads = qkv_weight.shape[1]
    score_scale = HEAD ** (-0.5)

    text_own = jnp.transpose(text_tokens[0], (1, 0, 2)).astype(jnp.float32)
    text_in = modulate(text_own, modifiers[:, 6], modifiers[:, 7]).astype(jnp.bfloat16)
    text_local = text_in.shape[0]
    row_idx = lax.axis_index("row")
    col_idx = lax.axis_index("col")
    if text_local % cols_n == 0 and cols_n & (cols_n - 1) == 0:
        sub = text_local // cols_n
        piece = lax.dynamic_slice_in_dim(text_in, col_idx * sub, sub, 0)
        joined = jnp.concatenate([image_tokens[0, 0], piece.reshape(sub * prompts, model_width)], 0)
        joined = lax.all_gather(joined, "row", axis=0, tiled=False)
        first_image = joined[:, :own_rows].reshape(-1, model_width)
        piece = joined[:, own_rows:].reshape(rows_n * sub, prompts, model_width)
        text_rows = gather_any_order(piece, "col")
        src_col = jnp.bitwise_xor(col_idx, jnp.arange(cols_n))
        positions = (
            src_col[:, None, None] * sub
            + jnp.arange(rows_n)[None, :, None] * text_local
            + jnp.arange(sub)[None, None, :]
        ).reshape(-1)
    else:
        text_rows = lax.all_gather(text_in, "row", axis=0, tiled=True)
        positions = jnp.arange(text_rows.shape[0])
        first_image = None
    text_count = text_rows.shape[0]
    text_proj = jnp.dot(
        text_rows.reshape(-1, model_width),
        text_kv_weight.reshape(model_width, -1),
        preferred_element_type=jnp.float32,
    )
    text_proj = text_proj.reshape(text_count, prompts, local_heads, 2 * HEAD)
    text_key = rms_norm(text_proj[..., :HEAD], qk_gains[2]).astype(jnp.bfloat16)
    text_value = text_proj[..., HEAD:].astype(jnp.bfloat16)
    text_valid = (positions[None, :] < text_lengths[0][:, None]).astype(jnp.float32)

    qkv_flat = qkv_weight.reshape(model_width, -1)
    out_flat = out_weight.reshape(local_heads * HEAD, model_width)
    velocities = []
    for p in range(prompts):
        mods = modifiers[p]
        if p == 0 and first_image is not None:
            image_rows = first_image
        else:
            image_rows = lax.all_gather(image_tokens[0, p], "row", axis=0, tiled=True)
        query_count = image_rows.shape[0]
        image_float = image_rows.astype(jnp.float32)
        image_in = modulate(image_float, mods[0], mods[1]).astype(jnp.bfloat16)
        projected = jnp.dot(image_in, qkv_flat, preferred_element_type=jnp.float32)
        projected = projected.reshape(query_count, local_heads, 3 * HEAD)
        queries = rms_norm(projected[..., :HEAD], qk_gains[0]).astype(jnp.bfloat16)
        image_key = rms_norm(projected[..., HEAD : 2 * HEAD], qk_gains[1]).astype(jnp.bfloat16)
        image_value = projected[..., 2 * HEAD :].astype(jnp.bfloat16)
        key_value = jnp.concatenate([image_key, image_value], axis=-1)
        all_pairs = gather_any_order(key_value, "col")
        image_weights = jnp.exp(
            jnp.einsum(
                "qhd,khd->hqk", queries, all_pairs[..., :HEAD], preferred_element_type=jnp.float32
            )
            * score_scale
        )
        text_weights = jnp.exp(
            jnp.einsum("qhd,khd->hqk", queries, text_key[:, p], preferred_element_type=jnp.float32)
            * score_scale
        )
        text_weights = text_weights * text_valid[p][None, None, :]
        denominator = jnp.sum(image_weights, axis=-1, keepdims=True) + jnp.sum(
            text_weights, axis=-1, keepdims=True
        )
        image_shares = (image_weights / denominator).astype(jnp.bfloat16)
        text_shares = (text_weights / denominator).astype(jnp.bfloat16)
        mixed = jnp.einsum(
            "hqk,khd->qhd", image_shares, all_pairs[..., HEAD:], preferred_element_type=jnp.float32
        )
        mixed = mixed + jnp.einsum(
            "hqk,khd->qhd", text_shares, text_value[:, p], preferred_element_type=jnp.float32
        )
        head_rows = mixed.astype(jnp.bfloat16).reshape(query_count, local_heads * HEAD)
        partial_value = jnp.dot(head_rows, out_flat, preferred_element_type=jnp.float32)
        attention = reduce_scatter_line(partial_value.astype(jnp.bfloat16), "row")
        mid_own = image_tokens[0, p].astype(jnp.float32) + mods[2] * attention
        normed_own = modulate(mid_own, mods[3], mods[4]).astype(jnp.bfloat16)
        normed = lax.all_gather(normed_own, "row", axis=0, tiled=True)
        hidden_units = jax.nn.gelu(
            jnp.dot(normed, up_weight, preferred_element_type=jnp.float32),
            approximate=True,
        ).astype(jnp.bfloat16)
        product = jnp.dot(hidden_units, down_weight, preferred_element_type=jnp.float32)
        feed = reduce_scatter_line(product.astype(jnp.bfloat16), "row")
        final_rows = mid_own + mods[5] * feed
        final_in = modulate(final_rows, mods[8], mods[9]).astype(jnp.bfloat16)
        velocities.append(jnp.dot(final_in, final_weight, preferred_element_type=jnp.float32))
    own_velocity = jnp.stack(velocities, axis=1)
    own_velocity = own_velocity.reshape(1, own_rows, prompts, -1)
    both_halves = lax.all_to_all(own_velocity, "cfg", split_axis=3, concat_axis=0, tiled=True)
    conditional = both_halves[0]
    unconditional = both_halves[1]
    guided = unconditional + guidance[0] * (conditional - unconditional)
    velocity = jnp.transpose(guided, (1, 0, 2))
    sigma_pair = lax.dynamic_slice_in_dim(sigmas, step_index[0], 2, 0)
    return (velocity, latents + (sigma_pair[1] - sigma_pair[0]) * velocity)


def solution(mesh):
    placed = (
        P("cfg", None, ("row", "col"), None),
        P("cfg", None, "row", None),
        P("cfg", None),
        P("cfg", None, None, None),
        P(),
        P(None, "row", None),
        P(None, "row", None),
        P("row", None, None),
        P(None, "row"),
        P("row", None),
        P(),
        P(None, ("row", "col"), "cfg"),
        P(),
        P(),
        P(),
    )
    return jax.shard_map(
        shards,
        mesh=mesh,
        in_specs=placed,
        out_specs=(P(None, ("row", "col"), "cfg"), P(None, ("row", "col"), "cfg")),
        check_vma=False,
    )
```

```python
import jax
import jax.numpy as jnp
from jax import lax
from jax.sharding import PartitionSpec as P

HEAD = 64


epsilon = 1e-06


def layer_norm(inputs):
    average = jnp.mean(inputs, axis=-1, keepdims=True)
    centered = inputs - average
    variance = jnp.mean(centered * centered, axis=-1, keepdims=True)
    return centered / jnp.sqrt(variance + epsilon)


def modulate(inputs, shifts, scales):
    return layer_norm(inputs) * (1.0 + scales) + shifts


def rms_norm(inputs, norm_gain):
    square_mean = jnp.mean(inputs * inputs, axis=-1, keepdims=True)
    return inputs / jnp.sqrt(square_mean + epsilon) * norm_gain


def power_of_two(n):
    return n & (n - 1) == 0


def gather_any_order(x, name):
    n = lax.axis_size(name)
    m = 1
    while m < n:
        pairs = [(i, i ^ m) for i in range(n)]
        x = jnp.concatenate([x, lax.ppermute(x, name, pairs)], axis=0)
        m *= 2
    return x


def shards(
    image_tokens,
    text_tokens,
    text_lengths,
    modulation,
    qk_gains,
    qkv_weight,
    text_kv_weight,
    out_weight,
    up_weight,
    down_weight,
    final_weight,
    latents,
    sigmas,
    step_index,
    guidance,
):
    modifiers = modulation[0]
    own_image = jnp.transpose(image_tokens[0], (1, 0, 2))
    own_rows = own_image.shape[0]
    prompts = own_image.shape[1]
    model_width = own_image.shape[2]
    rows_n = lax.axis_size("row")
    cols_n = lax.axis_size("col")
    row_idx = lax.axis_index("row")
    col_idx = lax.axis_index("col")
    local_heads = qkv_weight.shape[1]
    score_scale = HEAD ** (-0.5)

    text_own = jnp.transpose(text_tokens[0], (1, 0, 2)).astype(jnp.float32)
    text_in = modulate(text_own, modifiers[:, 6], modifiers[:, 7]).astype(jnp.bfloat16)
    text_local = text_in.shape[0]
    if text_local % cols_n == 0 and power_of_two(cols_n):
        sub = text_local // cols_n
        piece = lax.dynamic_slice_in_dim(text_in, col_idx * sub, sub, 0)
        joined = lax.all_gather(
            jnp.concatenate([own_image, piece], axis=0), "row", axis=0, tiled=False
        )
        image_rows = joined[:, :own_rows]
        text_rows = gather_any_order(joined[:, own_rows:].reshape(-1, prompts, model_width), "col")
        src_col = jnp.bitwise_xor(col_idx, jnp.arange(cols_n))
        positions = (
            src_col[:, None, None] * sub
            + jnp.arange(rows_n)[None, :, None] * text_local
            + jnp.arange(sub)[None, None, :]
        ).reshape(-1)
    else:
        image_rows = lax.all_gather(own_image, "row", axis=0, tiled=False)
        text_rows = lax.all_gather(text_in, "row", axis=0, tiled=True)
        positions = jnp.arange(text_rows.shape[0])
    image_float = image_rows.astype(jnp.float32)
    image_rows = image_rows.reshape(-1, prompts, model_width)
    query_count = image_rows.shape[0]
    image_in = modulate(
        image_rows.astype(jnp.float32), modifiers[:, 0], modifiers[:, 1]
    ).astype(jnp.bfloat16)
    projected = jnp.dot(
        image_in.reshape(-1, model_width),
        qkv_weight.reshape(model_width, -1),
        preferred_element_type=jnp.float32,
    )
    projected = projected.reshape(query_count, prompts, local_heads, 3 * HEAD)
    queries = rms_norm(projected[..., :HEAD], qk_gains[0]).astype(jnp.bfloat16)
    image_key = rms_norm(projected[..., HEAD : 2 * HEAD], qk_gains[1]).astype(jnp.bfloat16)
    image_value = projected[..., 2 * HEAD :].astype(jnp.bfloat16)
    key_value = jnp.concatenate([image_key, image_value], axis=-1)

    text_count = text_rows.shape[0]
    text_proj = jnp.dot(
        text_rows.reshape(-1, model_width),
        text_kv_weight.reshape(model_width, -1),
        preferred_element_type=jnp.float32,
    )
    text_proj = text_proj.reshape(text_count, prompts, local_heads, 2 * HEAD)
    text_key = rms_norm(text_proj[..., :HEAD], qk_gains[2]).astype(jnp.bfloat16)
    text_value = text_proj[..., HEAD:].astype(jnp.bfloat16)
    text_valid = (positions[None, :] < text_lengths[0][:, None]).astype(jnp.float32)

    def attend(keys, values, valid=None):
        weights = jnp.exp(
            jnp.einsum("qphd,kphd->phqk", queries, keys, preferred_element_type=jnp.float32)
            * score_scale
        )
        if valid is not None:
            weights = weights * valid[:, None, None, :]
        total = jnp.sum(weights, axis=-1)
        mixed = jnp.einsum(
            "phqk,kphd->qphd",
            weights.astype(jnp.bfloat16),
            values,
            preferred_element_type=jnp.float32,
        )
        return mixed, total

    mixed, total = attend(text_key, text_value, text_valid)
    if power_of_two(cols_n):
        held = key_value
        fresh = key_value
        m = 1
        while True:
            arriving = None
            if m < cols_n:
                arriving = lax.ppermute(held, "col", [(i, i ^ m) for i in range(cols_n)])
            part_mixed, part_total = attend(fresh[..., :HEAD], fresh[..., HEAD:])
            mixed = mixed + part_mixed
            total = total + part_total
            if arriving is None:
                break
            held = jnp.concatenate([held, arriving], axis=0)
            fresh = arriving
            m *= 2
    else:
        all_pairs = lax.all_gather(key_value, "col", axis=0, tiled=True)
        part_mixed, part_total = attend(all_pairs[..., :HEAD], all_pairs[..., HEAD:])
        mixed = mixed + part_mixed
        total = total + part_total
    head_out = mixed / jnp.transpose(total, (2, 0, 1))[..., None]
    head_rows = head_out.astype(jnp.bfloat16).reshape(query_count * prompts, local_heads * HEAD)
    out_flat = out_weight.reshape(local_heads * HEAD, model_width)
    partial_value = jnp.dot(head_rows, out_flat, preferred_element_type=jnp.float32)
    partial_value = partial_value.astype(jnp.bfloat16).reshape(rows_n, own_rows, prompts, model_width)

    streams = 2 if own_rows % 2 == 0 else 1
    part = own_rows // streams
    finals = []
    previous = None
    for s in range(streams):
        piece_value = partial_value[:, s * part : (s + 1) * part].reshape(-1, prompts, model_width)
        if previous is not None:
            piece_value, _ = lax.optimization_barrier((piece_value, previous))
        attention = lax.psum(piece_value, "row")
        previous = attention
        attention = attention.astype(jnp.float32)
        mid_rows = (
            image_float[:, s * part : (s + 1) * part].reshape(-1, prompts, model_width)
            + modifiers[:, 2] * attention
        )
        normed = modulate(mid_rows, modifiers[:, 3], modifiers[:, 4]).astype(jnp.bfloat16)
        hidden_units = jax.nn.gelu(
            jnp.dot(normed.reshape(-1, model_width), up_weight, preferred_element_type=jnp.float32),
            approximate=True,
        ).astype(jnp.bfloat16)
        product = jnp.dot(hidden_units, down_weight, preferred_element_type=jnp.float32)
        feed = lax.psum_scatter(
            product.reshape(rows_n * part, prompts, model_width).astype(jnp.bfloat16),
            "row",
            scatter_dimension=0,
            tiled=True,
        ).astype(jnp.float32)
        mid_own = lax.dynamic_index_in_dim(
            mid_rows.reshape(rows_n, part, prompts, model_width), row_idx, 0, keepdims=False
        )
        finals.append(mid_own + modifiers[:, 5] * feed)
    final_rows = jnp.concatenate(finals, axis=0)
    final_in = modulate(final_rows, modifiers[:, 8], modifiers[:, 9]).astype(jnp.bfloat16)
    own_velocity = jnp.dot(
        final_in.reshape(-1, model_width), final_weight, preferred_element_type=jnp.float32
    )
    own_velocity = own_velocity.reshape(1, own_rows, prompts, -1)
    both_halves = lax.all_to_all(own_velocity, "cfg", split_axis=3, concat_axis=0, tiled=True)
    conditional = both_halves[0]
    unconditional = both_halves[1]
    guided = unconditional + guidance[0] * (conditional - unconditional)
    velocity = jnp.transpose(guided, (1, 0, 2))
    sigma_pair = lax.dynamic_slice_in_dim(sigmas, step_index[0], 2, 0)
    return (velocity, latents + (sigma_pair[1] - sigma_pair[0]) * velocity)


def solution(mesh):
    placed = (
        P("cfg", None, ("row", "col"), None),
        P("cfg", None, "row", None),
        P("cfg", None),
        P("cfg", None, None, None),
        P(),
        P(None, "row", None),
        P(None, "row", None),
        P("row", None, None),
        P(None, "row"),
        P("row", None),
        P(),
        P(None, ("row", "col"), "cfg"),
        P(),
        P(),
        P(),
    )
    return jax.shard_map(
        shards,
        mesh=mesh,
        in_specs=placed,
        out_specs=(P(None, ("row", "col"), "cfg"), P(None, ("row", "col"), "cfg")),
        check_vma=False,
    )
```

```python
import jax
import jax.numpy as jnp
from jax import lax
from jax.sharding import PartitionSpec as P

HEAD = 64


epsilon = 1e-06


def layer_norm(inputs):
    average = jnp.mean(inputs, axis=-1, keepdims=True)
    centered = inputs - average
    variance = jnp.mean(centered * centered, axis=-1, keepdims=True)
    return centered / jnp.sqrt(variance + epsilon)


def modulate(inputs, shifts, scales):
    return layer_norm(inputs) * (1.0 + scales) + shifts


def rms_norm(inputs, norm_gain):
    square_mean = jnp.mean(inputs * inputs, axis=-1, keepdims=True)
    return inputs / jnp.sqrt(square_mean + epsilon) * norm_gain


def shards(
    image_tokens,
    text_tokens,
    text_lengths,
    modulation,
    qk_gains,
    qkv_weight,
    text_kv_weight,
    out_weight,
    up_weight,
    down_weight,
    final_weight,
    latents,
    sigmas,
    step_index,
    guidance,
):
    modifiers = modulation[0][:, :, None, :]
    own_image = image_tokens[0]
    prompts = own_image.shape[0]
    own_rows = own_image.shape[1]
    model_width = own_image.shape[2]
    text_own = text_tokens[0].astype(jnp.float32)
    text_in = modulate(text_own, modifiers[:, 6], modifiers[:, 7]).astype(jnp.bfloat16)
    image_rows = lax.all_gather(own_image, "row", axis=1, tiled=True)
    text_rows = lax.all_gather(text_in, "row", axis=1, tiled=True)
    query_count = image_rows.shape[1]
    image_float = image_rows.astype(jnp.float32)
    image_in = modulate(image_float, modifiers[:, 0], modifiers[:, 1]).astype(jnp.bfloat16)
    local_heads = qkv_weight.shape[1]
    projected = jnp.dot(
        image_in.reshape(-1, model_width),
        qkv_weight.reshape(model_width, -1),
        preferred_element_type=jnp.float32,
    )
    projected = projected.reshape(prompts, query_count, local_heads, 3 * HEAD)
    queries = rms_norm(projected[..., :HEAD], qk_gains[0]).astype(jnp.bfloat16)
    image_key = rms_norm(projected[..., HEAD : 2 * HEAD], qk_gains[1]).astype(jnp.bfloat16)
    image_value = projected[..., 2 * HEAD :].astype(jnp.bfloat16)
    key_value = jnp.concatenate([image_key, image_value], axis=-1)
    all_pairs = lax.all_gather(key_value, "col", axis=1, tiled=True)
    text_count = text_rows.shape[1]
    text_proj = jnp.dot(
        text_rows.reshape(-1, model_width),
        text_kv_weight.reshape(model_width, -1),
        preferred_element_type=jnp.float32,
    )
    text_proj = text_proj.reshape(prompts, text_count, local_heads, 2 * HEAD)
    text_key = rms_norm(text_proj[..., :HEAD], qk_gains[2]).astype(jnp.bfloat16)
    text_value = text_proj[..., HEAD:].astype(jnp.bfloat16)
    text_valid = (jnp.arange(text_count)[None, :] < text_lengths[0][:, None]).astype(jnp.float32)
    score_scale = HEAD ** (-0.5)
    image_weights = jnp.exp(
        jnp.einsum(
            "pqhd,pkhd->phqk", queries, all_pairs[..., :HEAD], preferred_element_type=jnp.float32
        )
        * score_scale
    )
    text_weights = jnp.exp(
        jnp.einsum("pqhd,pkhd->phqk", queries, text_key, preferred_element_type=jnp.float32)
        * score_scale
    )
    text_weights = text_weights * text_valid[:, None, None, :]
    denominator = jnp.sum(image_weights, axis=-1, keepdims=True) + jnp.sum(
        text_weights, axis=-1, keepdims=True
    )
    image_shares = (image_weights / denominator).astype(jnp.bfloat16)
    text_shares = (text_weights / denominator).astype(jnp.bfloat16)
    mixed = jnp.einsum(
        "phqk,pkhd->pqhd", image_shares, all_pairs[..., HEAD:], preferred_element_type=jnp.float32
    )
    mixed = mixed + jnp.einsum(
        "phqk,pkhd->pqhd", text_shares, text_value, preferred_element_type=jnp.float32
    )
    head_rows = mixed.astype(jnp.bfloat16).reshape(prompts * query_count, local_heads * HEAD)
    out_flat = out_weight.reshape(local_heads * HEAD, model_width)
    partial_value = jnp.dot(head_rows, out_flat, preferred_element_type=jnp.float32)
    attention = lax.psum(
        partial_value.reshape(prompts, query_count, model_width).astype(jnp.bfloat16), "row"
    ).astype(jnp.float32)
    mid_rows = image_float + modifiers[:, 2] * attention
    normed = modulate(mid_rows, modifiers[:, 3], modifiers[:, 4]).astype(jnp.bfloat16)
    hidden_units = jax.nn.gelu(
        jnp.dot(normed.reshape(-1, model_width), up_weight, preferred_element_type=jnp.float32),
        approximate=True,
    ).astype(jnp.bfloat16)
    mid_own = lax.dynamic_slice_in_dim(mid_rows, lax.axis_index("row") * own_rows, own_rows, 1)
    product = jnp.dot(hidden_units, down_weight, preferred_element_type=jnp.float32)
    feed = lax.psum_scatter(
        product.reshape(prompts, query_count, model_width).astype(jnp.bfloat16),
        "row",
        scatter_dimension=1,
        tiled=True,
    ).astype(jnp.float32)
    final_rows = mid_own + modifiers[:, 5] * feed
    final_in = modulate(final_rows, modifiers[:, 8], modifiers[:, 9]).astype(jnp.bfloat16)
    own_velocity = jnp.dot(
        final_in.reshape(-1, model_width), final_weight, preferred_element_type=jnp.float32
    )
    own_velocity = own_velocity.reshape(1, prompts, own_rows, -1)
    both_halves = lax.all_to_all(own_velocity, "cfg", split_axis=3, concat_axis=0, tiled=True)
    conditional = both_halves[0]
    unconditional = both_halves[1]
    velocity = unconditional + guidance[0] * (conditional - unconditional)
    sigma_pair = lax.dynamic_slice_in_dim(sigmas, step_index[0], 2, 0)
    return (velocity, latents + (sigma_pair[1] - sigma_pair[0]) * velocity)


def solution(mesh):
    placed = (
        P("cfg", None, ("row", "col"), None),
        P("cfg", None, "row", None),
        P("cfg", None),
        P("cfg", None, None, None),
        P(),
        P(None, "row", None),
        P(None, "row", None),
        P("row", None, None),
        P(None, "row"),
        P("row", None),
        P(),
        P(None, ("row", "col"), "cfg"),
        P(),
        P(),
        P(),
    )
    return jax.shard_map(
        shards,
        mesh=mesh,
        in_specs=placed,
        out_specs=(P(None, ("row", "col"), "cfg"), P(None, ("row", "col"), "cfg")),
        check_vma=False,
    )
```

```python
import jax
import jax.numpy as jnp
from jax import lax
from jax.sharding import PartitionSpec as P

HEAD = 64


epsilon = 1e-06


def layer_norm(inputs):
    average = jnp.mean(inputs, axis=-1, keepdims=True)
    centered = inputs - average
    variance = jnp.mean(centered * centered, axis=-1, keepdims=True)
    return centered / jnp.sqrt(variance + epsilon)


def modulate(inputs, shifts, scales):
    return layer_norm(inputs) * (1.0 + scales) + shifts


def rms_norm(inputs, norm_gain):
    square_mean = jnp.mean(inputs * inputs, axis=-1, keepdims=True)
    return inputs / jnp.sqrt(square_mean + epsilon) * norm_gain


def shards(
    image_tokens,
    text_tokens,
    text_lengths,
    modulation,
    qk_gains,
    qkv_weight,
    text_kv_weight,
    out_weight,
    up_weight,
    down_weight,
    final_weight,
    latents,
    sigmas,
    step_index,
    guidance,
):
    modifiers = modulation[0][:, :, None, :]
    own_image = image_tokens[0]
    prompts = own_image.shape[0]
    own_rows = own_image.shape[1]
    model_width = own_image.shape[2]
    text_own = text_tokens[0].astype(jnp.float32)
    text_in = modulate(text_own, modifiers[:, 6], modifiers[:, 7]).astype(jnp.bfloat16)
    rows_n = lax.axis_size("row")
    cols_n = lax.axis_size("col")
    col_idx = lax.axis_index("col")
    text_local = text_in.shape[1]
    lanes = 128
    folded = text_local % cols_n == 0 and model_width % lanes == 0
    if folded:
        sub = text_local // cols_n
        piece = lax.dynamic_slice_in_dim(text_in, col_idx * sub, sub, 1)
        joined = lax.all_gather(
            jnp.concatenate([own_image, piece], axis=1), "row", axis=1, tiled=True
        ).reshape(prompts, rows_n, own_rows + sub, model_width)
        image_rows = joined[:, :, :own_rows].reshape(prompts, rows_n * own_rows, model_width)
        text_piece = joined[:, :, own_rows:].reshape(prompts, -1, lanes)
    else:
        image_rows = lax.all_gather(own_image, "row", axis=1, tiled=True)
        text_rows = lax.all_gather(text_in, "row", axis=1, tiled=True)
    query_count = image_rows.shape[1]
    image_float = image_rows.astype(jnp.float32)
    image_in = modulate(image_float, modifiers[:, 0], modifiers[:, 1]).astype(jnp.bfloat16)
    local_heads = qkv_weight.shape[1]
    projected = jnp.dot(
        image_in.reshape(-1, model_width),
        qkv_weight.reshape(model_width, -1),
        preferred_element_type=jnp.float32,
    )
    projected = projected.reshape(prompts, query_count, local_heads, 3 * HEAD)
    queries = rms_norm(projected[..., :HEAD], qk_gains[0]).astype(jnp.bfloat16)
    image_key = rms_norm(projected[..., HEAD : 2 * HEAD], qk_gains[1]).astype(jnp.bfloat16)
    image_value = projected[..., 2 * HEAD :].astype(jnp.bfloat16)
    key_value = jnp.concatenate([image_key, image_value], axis=-1)
    if folded:
        kv_flat = key_value.reshape(prompts, -1, lanes)
        both = lax.all_gather(
            jnp.concatenate([kv_flat, text_piece], axis=1), "col", axis=1, tiled=True
        ).reshape(prompts, cols_n, kv_flat.shape[1] + text_piece.shape[1], lanes)
        all_pairs = both[:, :, : kv_flat.shape[1]].reshape(
            prompts, cols_n * query_count, local_heads, 2 * HEAD
        )
        text_rows = both[:, :, kv_flat.shape[1] :].reshape(prompts, -1, model_width)
        positions = (
            jnp.arange(cols_n)[:, None, None] * sub
            + jnp.arange(rows_n)[None, :, None] * text_local
            + jnp.arange(sub)[None, None, :]
        ).reshape(-1)
    else:
        all_pairs = lax.all_gather(key_value, "col", axis=1, tiled=True)
        positions = jnp.arange(text_rows.shape[1])
    text_count = text_rows.shape[1]
    text_proj = jnp.dot(
        text_rows.reshape(-1, model_width),
        text_kv_weight.reshape(model_width, -1),
        preferred_element_type=jnp.float32,
    )
    text_proj = text_proj.reshape(prompts, text_count, local_heads, 2 * HEAD)
    text_key = rms_norm(text_proj[..., :HEAD], qk_gains[2]).astype(jnp.bfloat16)
    text_value = text_proj[..., HEAD:].astype(jnp.bfloat16)
    text_valid = (positions[None, :] < text_lengths[0][:, None]).astype(jnp.float32)
    score_scale = HEAD ** (-0.5)
    image_weights = jnp.exp(
        jnp.einsum(
            "pqhd,pkhd->phqk", queries, all_pairs[..., :HEAD], preferred_element_type=jnp.float32
        )
        * score_scale
    )
    text_weights = jnp.exp(
        jnp.einsum("pqhd,pkhd->phqk", queries, text_key, preferred_element_type=jnp.float32)
        * score_scale
    )
    text_weights = text_weights * text_valid[:, None, None, :]
    denominator = jnp.sum(image_weights, axis=-1, keepdims=True) + jnp.sum(
        text_weights, axis=-1, keepdims=True
    )
    image_shares = (image_weights / denominator).astype(jnp.bfloat16)
    text_shares = (text_weights / denominator).astype(jnp.bfloat16)
    mixed = jnp.einsum(
        "phqk,pkhd->pqhd", image_shares, all_pairs[..., HEAD:], preferred_element_type=jnp.float32
    )
    mixed = mixed + jnp.einsum(
        "phqk,pkhd->pqhd", text_shares, text_value, preferred_element_type=jnp.float32
    )
    head_rows = mixed.astype(jnp.bfloat16).reshape(prompts * query_count, local_heads * HEAD)
    out_flat = out_weight.reshape(local_heads * HEAD, model_width)
    partial_value = jnp.dot(head_rows, out_flat, preferred_element_type=jnp.float32)
    attention = lax.psum(
        partial_value.reshape(prompts, query_count, model_width).astype(jnp.bfloat16), "row"
    ).astype(jnp.float32)
    mid_rows = image_float + modifiers[:, 2] * attention
    normed = modulate(mid_rows, modifiers[:, 3], modifiers[:, 4]).astype(jnp.bfloat16)
    hidden_units = jax.nn.gelu(
        jnp.dot(normed.reshape(-1, model_width), up_weight, preferred_element_type=jnp.float32),
        approximate=True,
    ).astype(jnp.bfloat16)
    mid_own = lax.dynamic_slice_in_dim(mid_rows, lax.axis_index("row") * own_rows, own_rows, 1)
    product = jnp.dot(hidden_units, down_weight, preferred_element_type=jnp.float32)
    feed = lax.psum_scatter(
        product.reshape(prompts, query_count, model_width).astype(jnp.bfloat16),
        "row",
        scatter_dimension=1,
        tiled=True,
    ).astype(jnp.float32)
    final_rows = mid_own + modifiers[:, 5] * feed
    final_in = modulate(final_rows, modifiers[:, 8], modifiers[:, 9]).astype(jnp.bfloat16)
    own_velocity = jnp.dot(
        final_in.reshape(-1, model_width), final_weight, preferred_element_type=jnp.float32
    )
    own_velocity = own_velocity.reshape(1, prompts, own_rows, -1)
    both_halves = lax.all_to_all(own_velocity, "cfg", split_axis=3, concat_axis=0, tiled=True)
    conditional = both_halves[0]
    unconditional = both_halves[1]
    velocity = unconditional + guidance[0] * (conditional - unconditional)
    sigma_pair = lax.dynamic_slice_in_dim(sigmas, step_index[0], 2, 0)
    return (velocity, latents + (sigma_pair[1] - sigma_pair[0]) * velocity)


def solution(mesh):
    placed = (
        P("cfg", None, ("row", "col"), None),
        P("cfg", None, "row", None),
        P("cfg", None),
        P("cfg", None, None, None),
        P(),
        P(None, "row", None),
        P(None, "row", None),
        P("row", None, None),
        P(None, "row"),
        P("row", None),
        P(),
        P(None, ("row", "col"), "cfg"),
        P(),
        P(),
        P(),
    )
    return jax.shard_map(
        shards,
        mesh=mesh,
        in_specs=placed,
        out_specs=(P(None, ("row", "col"), "cfg"), P(None, ("row", "col"), "cfg")),
        check_vma=False,
    )
```

```python
import jax
import jax.numpy as jnp
from jax import lax
from jax.sharding import PartitionSpec as P

HEAD = 64


epsilon = 1e-06


def layer_norm(inputs):
    average = jnp.mean(inputs, axis=-1, keepdims=True)
    centered = inputs - average
    variance = jnp.mean(centered * centered, axis=-1, keepdims=True)
    return centered / jnp.sqrt(variance + epsilon)


def modulate(inputs, shifts, scales):
    return layer_norm(inputs) * (1.0 + scales) + shifts


def rms_norm(inputs, norm_gain):
    square_mean = jnp.mean(inputs * inputs, axis=-1, keepdims=True)
    return inputs / jnp.sqrt(square_mean + epsilon) * norm_gain


def line_gather(x, name, axis):
    n = lax.axis_size(name)
    me = lax.axis_index(name)
    blocks = [x]
    sources = [me]
    up = x
    down = x
    for s in range(1, n):
        up = lax.ppermute(up, name, [(k, k + 1) for k in range(n - 1)])
        down = lax.ppermute(down, name, [(k + 1, k) for k in range(n - 1)])
        blocks += [up, down]
        sources += [jnp.where(me - s >= 0, me - s, -1), jnp.where(me + s < n, me + s, -1)]
    return jnp.concatenate(blocks, axis=axis), jnp.stack(sources)


def shards(
    image_tokens,
    text_tokens,
    text_lengths,
    modulation,
    qk_gains,
    qkv_weight,
    text_kv_weight,
    out_weight,
    up_weight,
    down_weight,
    final_weight,
    latents,
    sigmas,
    step_index,
    guidance,
):
    modifiers = modulation[0][:, :, None, :]
    own_image = image_tokens[0]
    prompts = own_image.shape[0]
    own_rows = own_image.shape[1]
    model_width = own_image.shape[2]
    text_own = text_tokens[0].astype(jnp.float32)
    text_in = modulate(text_own, modifiers[:, 6], modifiers[:, 7]).astype(jnp.bfloat16)
    image_rows = lax.all_gather(own_image, "row", axis=1, tiled=True)
    text_local = text_in.shape[1]
    if lax.axis_size("row") <= 4:
        text_rows, sources = line_gather(text_in, "row", 1)
        positions = jnp.where(
            sources[:, None] >= 0,
            sources[:, None] * text_local + jnp.arange(text_local)[None, :],
            jnp.iinfo(jnp.int32).max,
        ).reshape(-1)
    else:
        text_rows = lax.all_gather(text_in, "row", axis=1, tiled=True)
        positions = jnp.arange(text_rows.shape[1])
    query_count = image_rows.shape[1]
    image_float = image_rows.astype(jnp.float32)
    image_in = modulate(image_float, modifiers[:, 0], modifiers[:, 1]).astype(jnp.bfloat16)
    local_heads = qkv_weight.shape[1]
    projected = jnp.dot(
        image_in.reshape(-1, model_width),
        qkv_weight.reshape(model_width, -1),
        preferred_element_type=jnp.float32,
    )
    projected = projected.reshape(prompts, query_count, local_heads, 3 * HEAD)
    queries = rms_norm(projected[..., :HEAD], qk_gains[0]).astype(jnp.bfloat16)
    image_key = rms_norm(projected[..., HEAD : 2 * HEAD], qk_gains[1]).astype(jnp.bfloat16)
    image_value = projected[..., 2 * HEAD :].astype(jnp.bfloat16)
    key_value = jnp.concatenate([image_key, image_value], axis=-1)
    all_pairs = lax.all_gather(key_value, "col", axis=1, tiled=True)
    text_count = text_rows.shape[1]
    text_proj = jnp.dot(
        text_rows.reshape(-1, model_width),
        text_kv_weight.reshape(model_width, -1),
        preferred_element_type=jnp.float32,
    )
    text_proj = text_proj.reshape(prompts, text_count, local_heads, 2 * HEAD)
    text_key = rms_norm(text_proj[..., :HEAD], qk_gains[2]).astype(jnp.bfloat16)
    text_value = text_proj[..., HEAD:].astype(jnp.bfloat16)
    text_valid = (positions[None, :] < text_lengths[0][:, None]).astype(jnp.float32)
    score_scale = HEAD ** (-0.5)
    image_weights = jnp.exp(
        jnp.einsum(
            "pqhd,pkhd->phqk", queries, all_pairs[..., :HEAD], preferred_element_type=jnp.float32
        )
        * score_scale
    )
    text_weights = jnp.exp(
        jnp.einsum("pqhd,pkhd->phqk", queries, text_key, preferred_element_type=jnp.float32)
        * score_scale
    )
    text_weights = text_weights * text_valid[:, None, None, :]
    denominator = jnp.sum(image_weights, axis=-1, keepdims=True) + jnp.sum(
        text_weights, axis=-1, keepdims=True
    )
    image_shares = (image_weights / denominator).astype(jnp.bfloat16)
    text_shares = (text_weights / denominator).astype(jnp.bfloat16)
    mixed = jnp.einsum(
        "phqk,pkhd->pqhd", image_shares, all_pairs[..., HEAD:], preferred_element_type=jnp.float32
    )
    mixed = mixed + jnp.einsum(
        "phqk,pkhd->pqhd", text_shares, text_value, preferred_element_type=jnp.float32
    )
    head_rows = mixed.astype(jnp.bfloat16).reshape(prompts * query_count, local_heads * HEAD)
    out_flat = out_weight.reshape(local_heads * HEAD, model_width)
    partial_value = jnp.dot(head_rows, out_flat, preferred_element_type=jnp.float32)
    attention = lax.psum(
        partial_value.reshape(prompts, query_count, model_width).astype(jnp.bfloat16), "row"
    ).astype(jnp.float32)
    mid_rows = image_float + modifiers[:, 2] * attention
    normed = modulate(mid_rows, modifiers[:, 3], modifiers[:, 4]).astype(jnp.bfloat16)
    hidden_units = jax.nn.gelu(
        jnp.dot(normed.reshape(-1, model_width), up_weight, preferred_element_type=jnp.float32),
        approximate=True,
    ).astype(jnp.bfloat16)
    mid_own = lax.dynamic_slice_in_dim(mid_rows, lax.axis_index("row") * own_rows, own_rows, 1)
    product = jnp.dot(hidden_units, down_weight, preferred_element_type=jnp.float32)
    feed = lax.psum_scatter(
        product.reshape(prompts, query_count, model_width).astype(jnp.bfloat16),
        "row",
        scatter_dimension=1,
        tiled=True,
    ).astype(jnp.float32)
    final_rows = mid_own + modifiers[:, 5] * feed
    final_in = modulate(final_rows, modifiers[:, 8], modifiers[:, 9]).astype(jnp.bfloat16)
    own_velocity = jnp.dot(
        final_in.reshape(-1, model_width), final_weight, preferred_element_type=jnp.float32
    )
    own_velocity = own_velocity.reshape(1, prompts, own_rows, -1)
    both_halves = lax.all_to_all(own_velocity, "cfg", split_axis=3, concat_axis=0, tiled=True)
    conditional = both_halves[0]
    unconditional = both_halves[1]
    velocity = unconditional + guidance[0] * (conditional - unconditional)
    sigma_pair = lax.dynamic_slice_in_dim(sigmas, step_index[0], 2, 0)
    return (velocity, latents + (sigma_pair[1] - sigma_pair[0]) * velocity)


def solution(mesh):
    placed = (
        P("cfg", None, ("row", "col"), None),
        P("cfg", None, "row", None),
        P("cfg", None),
        P("cfg", None, None, None),
        P(),
        P(None, "row", None),
        P(None, "row", None),
        P("row", None, None),
        P(None, "row"),
        P("row", None),
        P(),
        P(None, ("row", "col"), "cfg"),
        P(),
        P(),
        P(),
    )
    return jax.shard_map(
        shards,
        mesh=mesh,
        in_specs=placed,
        out_specs=(P(None, ("row", "col"), "cfg"), P(None, ("row", "col"), "cfg")),
        check_vma=False,
    )
```

```python
import jax
import jax.numpy as jnp
from jax import lax
from jax.sharding import PartitionSpec as P

HEAD = 64


epsilon = 1e-06


def layer_norm(inputs):
    average = jnp.mean(inputs, axis=-1, keepdims=True)
    centered = inputs - average
    variance = jnp.mean(centered * centered, axis=-1, keepdims=True)
    return centered / jnp.sqrt(variance + epsilon)


def modulate(inputs, shifts, scales):
    return layer_norm(inputs) * (1.0 + scales) + shifts


def rms_norm(inputs, norm_gain):
    square_mean = jnp.mean(inputs * inputs, axis=-1, keepdims=True)
    return inputs / jnp.sqrt(square_mean + epsilon) * norm_gain


def line_gather(x, name, axis):
    n = lax.axis_size(name)
    me = lax.axis_index(name)
    blocks = [x]
    sources = [me]
    up = x
    down = x
    for s in range(1, n):
        up = lax.ppermute(up, name, [(k, k + 1) for k in range(n - 1)])
        down = lax.ppermute(down, name, [(k + 1, k) for k in range(n - 1)])
        blocks += [up, down]
        sources += [jnp.where(me - s >= 0, me - s, -1), jnp.where(me + s < n, me + s, -1)]
    return jnp.concatenate(blocks, axis=axis), jnp.stack(sources)


def shards(
    image_tokens,
    text_tokens,
    text_lengths,
    modulation,
    qk_gains,
    qkv_weight,
    text_kv_weight,
    out_weight,
    up_weight,
    down_weight,
    final_weight,
    latents,
    sigmas,
    step_index,
    guidance,
):
    modifiers = modulation[0][:, :, None, :]
    own_image = image_tokens[0]
    prompts = own_image.shape[0]
    own_rows = own_image.shape[1]
    model_width = own_image.shape[2]
    text_own = text_tokens[0].astype(jnp.float32)
    text_in = modulate(text_own, modifiers[:, 6], modifiers[:, 7]).astype(jnp.bfloat16)
    image_rows = lax.all_gather(own_image, "row", axis=1, tiled=True)
    text_local = text_in.shape[1]
    if lax.axis_size("row") <= 4:
        text_rows, sources = line_gather(text_in, "row", 1)
        positions = jnp.where(
            sources[:, None] >= 0,
            sources[:, None] * text_local + jnp.arange(text_local)[None, :],
            jnp.iinfo(jnp.int32).max,
        ).reshape(-1)
    else:
        text_rows = lax.all_gather(text_in, "row", axis=1, tiled=True)
        positions = jnp.arange(text_rows.shape[1])
    query_count = image_rows.shape[1]
    image_float = image_rows.astype(jnp.float32)
    image_in = modulate(image_float, modifiers[:, 0], modifiers[:, 1]).astype(jnp.bfloat16)
    local_heads = qkv_weight.shape[1]
    projected = jnp.dot(
        image_in.reshape(-1, model_width),
        qkv_weight.reshape(model_width, -1),
        preferred_element_type=jnp.float32,
    )
    projected = projected.reshape(prompts, query_count, local_heads, 3 * HEAD)
    queries = rms_norm(projected[..., :HEAD], qk_gains[0]).astype(jnp.bfloat16)
    image_key = rms_norm(projected[..., HEAD : 2 * HEAD], qk_gains[1]).astype(jnp.bfloat16)
    image_value = projected[..., 2 * HEAD :].astype(jnp.bfloat16)
    key_value = jnp.concatenate([image_key, image_value], axis=-1)
    all_pairs = lax.all_gather(key_value, "col", axis=1, tiled=True)
    text_count = text_rows.shape[1]
    text_proj = jnp.dot(
        text_rows.reshape(-1, model_width),
        text_kv_weight.reshape(model_width, -1),
        preferred_element_type=jnp.float32,
    )
    text_proj = text_proj.reshape(prompts, text_count, local_heads, 2 * HEAD)
    text_key = rms_norm(text_proj[..., :HEAD], qk_gains[2]).astype(jnp.bfloat16)
    text_value = text_proj[..., HEAD:].astype(jnp.bfloat16)
    text_valid = (positions[None, :] < text_lengths[0][:, None]).astype(jnp.float32)
    score_scale = HEAD ** (-0.5)
    image_weights = jnp.exp(
        jnp.einsum(
            "pqhd,pkhd->phqk", queries, all_pairs[..., :HEAD], preferred_element_type=jnp.float32
        )
        * score_scale
    )
    text_weights = jnp.exp(
        jnp.einsum("pqhd,pkhd->phqk", queries, text_key, preferred_element_type=jnp.float32)
        * score_scale
    )
    text_weights = text_weights * text_valid[:, None, None, :]
    denominator = jnp.sum(image_weights, axis=-1, keepdims=True) + jnp.sum(
        text_weights, axis=-1, keepdims=True
    )
    image_shares = (image_weights / denominator).astype(jnp.bfloat16)
    text_shares = (text_weights / denominator).astype(jnp.bfloat16)
    mixed = jnp.einsum(
        "phqk,pkhd->pqhd", image_shares, all_pairs[..., HEAD:], preferred_element_type=jnp.float32
    )
    mixed = mixed + jnp.einsum(
        "phqk,pkhd->pqhd", text_shares, text_value, preferred_element_type=jnp.float32
    )
    head_rows = mixed.astype(jnp.bfloat16).reshape(prompts * query_count, local_heads * HEAD)
    out_flat = out_weight.reshape(local_heads * HEAD, model_width)
    partial_value = jnp.dot(head_rows, out_flat, preferred_element_type=jnp.float32)
    rows_n = lax.axis_size("row")
    row_idx = lax.axis_index("row")
    partial_value = partial_value.astype(jnp.bfloat16).reshape(prompts, rows_n, own_rows, model_width)
    image_split = image_float.reshape(prompts, rows_n, own_rows, model_width)
    streams = 2 if own_rows % 2 == 0 else 1
    part = own_rows // streams

    def take(x, s):
        return x[:, :, s * part : (s + 1) * part].reshape(prompts, rows_n * part, model_width)

    attentions = []
    for s in range(streams):
        piece_value = take(partial_value, s)
        if attentions:
            piece_value, _ = lax.optimization_barrier((piece_value, attentions[-1]))
        attentions.append(lax.psum(piece_value, "row"))
    finals = []
    for s in range(streams):
        mid_rows = take(image_split, s) + modifiers[:, 2] * attentions[s].astype(jnp.float32)
        normed = modulate(mid_rows, modifiers[:, 3], modifiers[:, 4]).astype(jnp.bfloat16)
        hidden_units = jax.nn.gelu(
            jnp.dot(normed.reshape(-1, model_width), up_weight, preferred_element_type=jnp.float32),
            approximate=True,
        ).astype(jnp.bfloat16)
        product = jnp.dot(hidden_units, down_weight, preferred_element_type=jnp.float32)
        product = product.reshape(prompts, rows_n * part, model_width).astype(jnp.bfloat16)
        if s + 1 < streams:
            product, attentions[s + 1] = lax.optimization_barrier((product, attentions[s + 1]))
        feed = lax.psum_scatter(product, "row", scatter_dimension=1, tiled=True).astype(jnp.float32)
        mid_own = lax.dynamic_index_in_dim(
            mid_rows.reshape(prompts, rows_n, part, model_width), row_idx, 1, keepdims=False
        )
        finals.append(mid_own + modifiers[:, 5] * feed)
    final_rows = jnp.concatenate(finals, axis=1)
    final_in = modulate(final_rows, modifiers[:, 8], modifiers[:, 9]).astype(jnp.bfloat16)
    own_velocity = jnp.dot(
        final_in.reshape(-1, model_width), final_weight, preferred_element_type=jnp.float32
    )
    own_velocity = own_velocity.reshape(1, prompts, own_rows, -1)
    both_halves = lax.all_to_all(own_velocity, "cfg", split_axis=3, concat_axis=0, tiled=True)
    conditional = both_halves[0]
    unconditional = both_halves[1]
    velocity = unconditional + guidance[0] * (conditional - unconditional)
    sigma_pair = lax.dynamic_slice_in_dim(sigmas, step_index[0], 2, 0)
    return (velocity, latents + (sigma_pair[1] - sigma_pair[0]) * velocity)


def solution(mesh):
    placed = (
        P("cfg", None, ("row", "col"), None),
        P("cfg", None, "row", None),
        P("cfg", None),
        P("cfg", None, None, None),
        P(),
        P(None, "row", None),
        P(None, "row", None),
        P("row", None, None),
        P(None, "row"),
        P("row", None),
        P(),
        P(None, ("row", "col"), "cfg"),
        P(),
        P(),
        P(),
    )
    return jax.shard_map(
        shards,
        mesh=mesh,
        in_specs=placed,
        out_specs=(P(None, ("row", "col"), "cfg"), P(None, ("row", "col"), "cfg")),
        check_vma=False,
    )
```

```python
import jax
import jax.numpy as jnp
from jax import lax
from jax.sharding import PartitionSpec as P

HEAD = 64


epsilon = 1e-06


def layer_norm(inputs):
    average = jnp.mean(inputs, axis=-1, keepdims=True)
    centered = inputs - average
    variance = jnp.mean(centered * centered, axis=-1, keepdims=True)
    return centered / jnp.sqrt(variance + epsilon)


def modulate(inputs, shifts, scales):
    return layer_norm(inputs) * (1.0 + scales) + shifts


def rms_norm(inputs, norm_gain):
    square_mean = jnp.mean(inputs * inputs, axis=-1, keepdims=True)
    return inputs / jnp.sqrt(square_mean + epsilon) * norm_gain


def line_gather(x, name, axis):
    n = lax.axis_size(name)
    me = lax.axis_index(name)
    blocks = [x]
    sources = [me]
    up = x
    down = x
    for s in range(1, n):
        up = lax.ppermute(up, name, [(k, k + 1) for k in range(n - 1)])
        down = lax.ppermute(down, name, [(k + 1, k) for k in range(n - 1)])
        blocks += [up, down]
        sources += [jnp.where(me - s >= 0, me - s, -1), jnp.where(me + s < n, me + s, -1)]
    return jnp.concatenate(blocks, axis=axis), jnp.stack(sources)


def shards(
    image_tokens,
    text_tokens,
    text_lengths,
    modulation,
    qk_gains,
    qkv_weight,
    text_kv_weight,
    out_weight,
    up_weight,
    down_weight,
    final_weight,
    latents,
    sigmas,
    step_index,
    guidance,
):
    modifiers = modulation[0][:, :, None, :]
    own_image = image_tokens[0]
    prompts = own_image.shape[0]
    own_rows = own_image.shape[1]
    model_width = own_image.shape[2]
    text_own = text_tokens[0].astype(jnp.float32)
    text_in = modulate(text_own, modifiers[:, 6], modifiers[:, 7]).astype(jnp.bfloat16)
    image_rows = lax.all_gather(own_image, "row", axis=1, tiled=True)
    text_local = text_in.shape[1]
    if lax.axis_size("row") <= 4:
        text_rows, sources = line_gather(text_in, "row", 1)
        positions = jnp.where(
            sources[:, None] >= 0,
            sources[:, None] * text_local + jnp.arange(text_local)[None, :],
            jnp.iinfo(jnp.int32).max,
        ).reshape(-1)
    else:
        text_rows = lax.all_gather(text_in, "row", axis=1, tiled=True)
        positions = jnp.arange(text_rows.shape[1])
    query_count = image_rows.shape[1]
    image_float = image_rows.astype(jnp.float32)
    image_in = modulate(image_float, modifiers[:, 0], modifiers[:, 1]).astype(jnp.bfloat16)
    local_heads = qkv_weight.shape[1]
    projected = jnp.dot(
        image_in.reshape(-1, model_width),
        qkv_weight.reshape(model_width, -1),
        preferred_element_type=jnp.float32,
    )
    projected = projected.reshape(prompts, query_count, local_heads, 3 * HEAD)
    queries = rms_norm(projected[..., :HEAD], qk_gains[0]).astype(jnp.bfloat16)
    image_key = rms_norm(projected[..., HEAD : 2 * HEAD], qk_gains[1]).astype(jnp.bfloat16)
    image_value = projected[..., 2 * HEAD :].astype(jnp.bfloat16)
    key_value = jnp.concatenate([image_key, image_value], axis=-1)
    all_pairs = lax.all_gather(key_value, "col", axis=1, tiled=True)
    text_count = text_rows.shape[1]
    text_proj = jnp.dot(
        text_rows.reshape(-1, model_width),
        text_kv_weight.reshape(model_width, -1),
        preferred_element_type=jnp.float32,
    )
    text_proj = text_proj.reshape(prompts, text_count, local_heads, 2 * HEAD)
    text_key = rms_norm(text_proj[..., :HEAD], qk_gains[2]).astype(jnp.bfloat16)
    text_value = text_proj[..., HEAD:].astype(jnp.bfloat16)
    text_valid = (positions[None, :] < text_lengths[0][:, None]).astype(jnp.float32)
    score_scale = HEAD ** (-0.5)
    rows_n = lax.axis_size("row")
    row_idx = lax.axis_index("row")
    image_split = image_float.reshape(prompts, rows_n, own_rows, model_width)
    streams = 2 if own_rows % 2 == 0 else 1
    part = own_rows // streams

    def take(x, s):
        return x[:, :, s * part : (s + 1) * part].reshape(prompts, rows_n * part, *x.shape[3:])

    score_scale = HEAD ** (-0.5)
    out_flat = out_weight.reshape(local_heads * HEAD, model_width)

    def attend(head_queries):
        image_weights = jnp.exp(
            jnp.einsum(
                "pqhd,pkhd->phqk",
                head_queries,
                all_pairs[..., :HEAD],
                preferred_element_type=jnp.float32,
            )
            * score_scale
        )
        text_weights = jnp.exp(
            jnp.einsum(
                "pqhd,pkhd->phqk", head_queries, text_key, preferred_element_type=jnp.float32
            )
            * score_scale
        )
        text_weights = text_weights * text_valid[:, None, None, :]
        denominator = jnp.sum(image_weights, axis=-1, keepdims=True) + jnp.sum(
            text_weights, axis=-1, keepdims=True
        )
        image_shares = (image_weights / denominator).astype(jnp.bfloat16)
        text_shares = (text_weights / denominator).astype(jnp.bfloat16)
        mixed = jnp.einsum(
            "phqk,pkhd->pqhd",
            image_shares,
            all_pairs[..., HEAD:],
            preferred_element_type=jnp.float32,
        )
        mixed = mixed + jnp.einsum(
            "phqk,pkhd->pqhd", text_shares, text_value, preferred_element_type=jnp.float32
        )
        count = head_queries.shape[1]
        head_rows = mixed.astype(jnp.bfloat16).reshape(prompts * count, local_heads * HEAD)
        partial_value = jnp.dot(head_rows, out_flat, preferred_element_type=jnp.float32)
        return partial_value.reshape(prompts, count, model_width).astype(jnp.bfloat16)

    query_split = queries.reshape(prompts, rows_n, own_rows, local_heads, HEAD)
    attentions = []
    piece_value = None
    for s in range(streams):
        head_queries = take(query_split, s)
        if piece_value is not None:
            head_queries, piece_value = lax.optimization_barrier((head_queries, piece_value))
            attentions.append(lax.psum(piece_value, "row"))
        next_value = attend(head_queries)
        if attentions:
            next_value, _ = lax.optimization_barrier((next_value, attentions[-1]))
        piece_value = next_value
    attentions.append(lax.psum(piece_value, "row"))
    finals = []
    for s in range(streams):
        mid_rows = take(image_split, s) + modifiers[:, 2] * attentions[s].astype(jnp.float32)
        normed = modulate(mid_rows, modifiers[:, 3], modifiers[:, 4]).astype(jnp.bfloat16)
        hidden_units = jax.nn.gelu(
            jnp.dot(normed.reshape(-1, model_width), up_weight, preferred_element_type=jnp.float32),
            approximate=True,
        ).astype(jnp.bfloat16)
        product = jnp.dot(hidden_units, down_weight, preferred_element_type=jnp.float32)
        product = product.reshape(prompts, rows_n * part, model_width).astype(jnp.bfloat16)
        if s + 1 < streams:
            product, attentions[s + 1] = lax.optimization_barrier((product, attentions[s + 1]))
        feed = lax.psum_scatter(product, "row", scatter_dimension=1, tiled=True).astype(jnp.float32)
        mid_own = lax.dynamic_index_in_dim(
            mid_rows.reshape(prompts, rows_n, part, model_width), row_idx, 1, keepdims=False
        )
        finals.append(mid_own + modifiers[:, 5] * feed)
    final_rows = jnp.concatenate(finals, axis=1)
    final_in = modulate(final_rows, modifiers[:, 8], modifiers[:, 9]).astype(jnp.bfloat16)
    own_velocity = jnp.dot(
        final_in.reshape(-1, model_width), final_weight, preferred_element_type=jnp.float32
    )
    own_velocity = own_velocity.reshape(1, prompts, own_rows, -1)
    both_halves = lax.all_to_all(own_velocity, "cfg", split_axis=3, concat_axis=0, tiled=True)
    conditional = both_halves[0]
    unconditional = both_halves[1]
    velocity = unconditional + guidance[0] * (conditional - unconditional)
    sigma_pair = lax.dynamic_slice_in_dim(sigmas, step_index[0], 2, 0)
    return (velocity, latents + (sigma_pair[1] - sigma_pair[0]) * velocity)


def solution(mesh):
    placed = (
        P("cfg", None, ("row", "col"), None),
        P("cfg", None, "row", None),
        P("cfg", None),
        P("cfg", None, None, None),
        P(),
        P(None, "row", None),
        P(None, "row", None),
        P("row", None, None),
        P(None, "row"),
        P("row", None),
        P(),
        P(None, ("row", "col"), "cfg"),
        P(),
        P(),
        P(),
    )
    return jax.shard_map(
        shards,
        mesh=mesh,
        in_specs=placed,
        out_specs=(P(None, ("row", "col"), "cfg"), P(None, ("row", "col"), "cfg")),
        check_vma=False,
    )
```

```python
import jax
import jax.numpy as jnp
from jax import lax
from jax.sharding import PartitionSpec as P

HEAD = 64


epsilon = 1e-06


def layer_norm(inputs):
    average = jnp.mean(inputs, axis=-1, keepdims=True)
    centered = inputs - average
    variance = jnp.mean(centered * centered, axis=-1, keepdims=True)
    return centered / jnp.sqrt(variance + epsilon)


def modulate(inputs, shifts, scales):
    return layer_norm(inputs) * (1.0 + scales) + shifts


def rms_norm(inputs, norm_gain):
    square_mean = jnp.mean(inputs * inputs, axis=-1, keepdims=True)
    return inputs / jnp.sqrt(square_mean + epsilon) * norm_gain


def line_gather(x, name, axis):
    n = lax.axis_size(name)
    me = lax.axis_index(name)
    blocks = [x]
    sources = [me]
    up = x
    down = x
    for s in range(1, n):
        up = lax.ppermute(up, name, [(k, k + 1) for k in range(n - 1)])
        down = lax.ppermute(down, name, [(k + 1, k) for k in range(n - 1)])
        blocks += [up, down]
        sources += [jnp.where(me - s >= 0, me - s, -1), jnp.where(me + s < n, me + s, -1)]
    return jnp.concatenate(blocks, axis=axis), jnp.stack(sources)


def shards(
    image_tokens,
    text_tokens,
    text_lengths,
    modulation,
    qk_gains,
    qkv_weight,
    text_kv_weight,
    out_weight,
    up_weight,
    down_weight,
    final_weight,
    latents,
    sigmas,
    step_index,
    guidance,
):
    modifiers = modulation[0][:, :, None, :]
    own_image = image_tokens[0]
    prompts = own_image.shape[0]
    own_rows = own_image.shape[1]
    model_width = own_image.shape[2]
    text_own = text_tokens[0].astype(jnp.float32)
    text_in = modulate(text_own, modifiers[:, 6], modifiers[:, 7]).astype(jnp.bfloat16)
    image_rows = lax.all_gather(own_image, "row", axis=1, tiled=True)
    text_local = text_in.shape[1]
    if lax.axis_size("row") <= 4:
        text_rows, sources = line_gather(text_in, "row", 1)
        positions = jnp.where(
            sources[:, None] >= 0,
            sources[:, None] * text_local + jnp.arange(text_local)[None, :],
            jnp.iinfo(jnp.int32).max,
        ).reshape(-1)
    else:
        text_rows = lax.all_gather(text_in, "row", axis=1, tiled=True)
        positions = jnp.arange(text_rows.shape[1])
    query_count = image_rows.shape[1]
    image_float = image_rows.astype(jnp.float32)
    image_in = modulate(image_float, modifiers[:, 0], modifiers[:, 1]).astype(jnp.bfloat16)
    local_heads = qkv_weight.shape[1]
    projected = jnp.dot(
        image_in.reshape(-1, model_width),
        qkv_weight.reshape(model_width, -1),
        preferred_element_type=jnp.float32,
    )
    projected = projected.reshape(prompts, query_count, local_heads, 3 * HEAD)
    queries = rms_norm(projected[..., :HEAD], qk_gains[0]).astype(jnp.bfloat16)
    image_key = rms_norm(projected[..., HEAD : 2 * HEAD], qk_gains[1]).astype(jnp.bfloat16)
    image_value = projected[..., 2 * HEAD :].astype(jnp.bfloat16)
    key_value = jnp.concatenate([image_key, image_value], axis=-1)
    all_pairs = lax.all_gather(key_value, "col", axis=1, tiled=True)
    text_count = text_rows.shape[1]
    text_proj = jnp.dot(
        text_rows.reshape(-1, model_width),
        text_kv_weight.reshape(model_width, -1),
        preferred_element_type=jnp.float32,
    )
    text_proj = text_proj.reshape(prompts, text_count, local_heads, 2 * HEAD)
    text_key = rms_norm(text_proj[..., :HEAD], qk_gains[2]).astype(jnp.bfloat16)
    text_value = text_proj[..., HEAD:].astype(jnp.bfloat16)
    text_valid = (positions[None, :] < text_lengths[0][:, None]).astype(jnp.float32)
    score_scale = HEAD ** (-0.5)
    rows_n = lax.axis_size("row")
    row_idx = lax.axis_index("row")
    image_split = image_float.reshape(prompts, rows_n, own_rows, model_width)
    streams = 2 if own_rows % 2 == 0 else 1
    part = own_rows // streams

    def take(x, s):
        return x[:, :, s * part : (s + 1) * part].reshape(prompts, rows_n * part, *x.shape[3:])

    score_scale = HEAD ** (-0.5)
    out_flat = out_weight.reshape(local_heads * HEAD, model_width)

    def attend(head_queries):
        image_weights = jnp.exp(
            jnp.einsum(
                "pqhd,pkhd->phqk",
                head_queries,
                all_pairs[..., :HEAD],
                preferred_element_type=jnp.float32,
            )
            * score_scale
        )
        text_weights = jnp.exp(
            jnp.einsum(
                "pqhd,pkhd->phqk", head_queries, text_key, preferred_element_type=jnp.float32
            )
            * score_scale
        )
        text_weights = text_weights * text_valid[:, None, None, :]
        denominator = jnp.sum(image_weights, axis=-1, keepdims=True) + jnp.sum(
            text_weights, axis=-1, keepdims=True
        )
        image_shares = (image_weights / denominator).astype(jnp.bfloat16)
        text_shares = (text_weights / denominator).astype(jnp.bfloat16)
        mixed = jnp.einsum(
            "phqk,pkhd->pqhd",
            image_shares,
            all_pairs[..., HEAD:],
            preferred_element_type=jnp.float32,
        )
        mixed = mixed + jnp.einsum(
            "phqk,pkhd->pqhd", text_shares, text_value, preferred_element_type=jnp.float32
        )
        count = head_queries.shape[1]
        head_rows = mixed.astype(jnp.bfloat16).reshape(prompts * count, local_heads * HEAD)
        partial_value = jnp.dot(head_rows, out_flat, preferred_element_type=jnp.float32)
        return partial_value.reshape(prompts, count, model_width).astype(jnp.bfloat16)

    query_split = queries.reshape(prompts, rows_n, own_rows, local_heads, HEAD)
    attentions = []
    piece_value = None
    for s in range(streams):
        head_queries = take(query_split, s)
        if piece_value is not None:
            head_queries, piece_value = lax.optimization_barrier((head_queries, piece_value))
            attentions.append(lax.psum(piece_value, "row"))
        next_value = attend(head_queries)
        if attentions:
            next_value, _ = lax.optimization_barrier((next_value, attentions[-1]))
        piece_value = next_value
    attentions.append(lax.psum(piece_value, "row"))
    finals = []
    for s in range(streams):
        mid_rows = take(image_split, s) + modifiers[:, 2] * attentions[s].astype(jnp.float32)
        normed = modulate(mid_rows, modifiers[:, 3], modifiers[:, 4]).astype(jnp.bfloat16)
        hidden_units = jax.nn.gelu(
            jnp.dot(normed.reshape(-1, model_width), up_weight, preferred_element_type=jnp.float32),
            approximate=True,
        ).astype(jnp.bfloat16)
        product = jnp.dot(hidden_units, down_weight, preferred_element_type=jnp.float32)
        product = product.reshape(prompts, rows_n * part, model_width).astype(jnp.bfloat16)
        if s + 1 < streams:
            product, attentions[s + 1] = lax.optimization_barrier((product, attentions[s + 1]))
        if finals:
            product, _ = lax.optimization_barrier((product, finals[-1]))
        feed = lax.psum_scatter(product, "row", scatter_dimension=1, tiled=True).astype(jnp.float32)
        mid_own = lax.dynamic_index_in_dim(
            mid_rows.reshape(prompts, rows_n, part, model_width), row_idx, 1, keepdims=False
        )
        finals.append(mid_own + modifiers[:, 5] * feed)
    final_rows = jnp.concatenate(finals, axis=1)
    final_in = modulate(final_rows, modifiers[:, 8], modifiers[:, 9]).astype(jnp.bfloat16)
    own_velocity = jnp.dot(
        final_in.reshape(-1, model_width), final_weight, preferred_element_type=jnp.float32
    )
    own_velocity = own_velocity.reshape(1, prompts, own_rows, -1)
    both_halves = lax.all_to_all(own_velocity, "cfg", split_axis=3, concat_axis=0, tiled=True)
    conditional = both_halves[0]
    unconditional = both_halves[1]
    velocity = unconditional + guidance[0] * (conditional - unconditional)
    sigma_pair = lax.dynamic_slice_in_dim(sigmas, step_index[0], 2, 0)
    return (velocity, latents + (sigma_pair[1] - sigma_pair[0]) * velocity)


def solution(mesh):
    placed = (
        P("cfg", None, ("row", "col"), None),
        P("cfg", None, "row", None),
        P("cfg", None),
        P("cfg", None, None, None),
        P(),
        P(None, "row", None),
        P(None, "row", None),
        P("row", None, None),
        P(None, "row"),
        P("row", None),
        P(),
        P(None, ("row", "col"), "cfg"),
        P(),
        P(),
        P(),
    )
    return jax.shard_map(
        shards,
        mesh=mesh,
        in_specs=placed,
        out_specs=(P(None, ("row", "col"), "cfg"), P(None, ("row", "col"), "cfg")),
        check_vma=False,
    )
```

```python
import jax
import jax.numpy as jnp
from jax import lax
from jax.sharding import PartitionSpec as P

HEAD = 64


epsilon = 1e-06


def layer_norm(inputs):
    average = jnp.mean(inputs, axis=-1, keepdims=True)
    centered = inputs - average
    variance = jnp.mean(centered * centered, axis=-1, keepdims=True)
    return centered / jnp.sqrt(variance + epsilon)


def modulate(inputs, shifts, scales):
    return layer_norm(inputs) * (1.0 + scales) + shifts


def rms_norm(inputs, norm_gain):
    square_mean = jnp.mean(inputs * inputs, axis=-1, keepdims=True)
    return inputs / jnp.sqrt(square_mean + epsilon) * norm_gain


def line_gather(x, name, axis):
    n = lax.axis_size(name)
    me = lax.axis_index(name)
    blocks = [x]
    sources = [me]
    up = x
    down = x
    for s in range(1, n):
        up = lax.ppermute(up, name, [(k, k + 1) for k in range(n - 1)])
        down = lax.ppermute(down, name, [(k + 1, k) for k in range(n - 1)])
        blocks += [up, down]
        sources += [jnp.where(me - s >= 0, me - s, -1), jnp.where(me + s < n, me + s, -1)]
    return jnp.concatenate(blocks, axis=axis), jnp.stack(sources)


def shards(
    image_tokens,
    text_tokens,
    text_lengths,
    modulation,
    qk_gains,
    qkv_weight,
    text_kv_weight,
    out_weight,
    up_weight,
    down_weight,
    final_weight,
    latents,
    sigmas,
    step_index,
    guidance,
):
    modifiers = modulation[0][:, :, None, :]
    own_image = image_tokens[0]
    prompts = own_image.shape[0]
    own_rows = own_image.shape[1]
    model_width = own_image.shape[2]
    text_own = text_tokens[0].astype(jnp.float32)
    text_in = modulate(text_own, modifiers[:, 6], modifiers[:, 7]).astype(jnp.bfloat16)
    image_rows = lax.all_gather(own_image, "row", axis=1, tiled=True)
    text_local = text_in.shape[1]
    if lax.axis_size("row") <= 4:
        text_rows, sources = line_gather(text_in, "row", 1)
        positions = jnp.where(
            sources[:, None] >= 0,
            sources[:, None] * text_local + jnp.arange(text_local)[None, :],
            jnp.iinfo(jnp.int32).max,
        ).reshape(-1)
    else:
        text_rows = lax.all_gather(text_in, "row", axis=1, tiled=True)
        positions = jnp.arange(text_rows.shape[1])
    query_count = image_rows.shape[1]
    image_float = image_rows.astype(jnp.float32)
    image_in = modulate(image_float, modifiers[:, 0], modifiers[:, 1]).astype(jnp.bfloat16)
    local_heads = qkv_weight.shape[1]
    projected = jnp.dot(
        image_in.reshape(-1, model_width),
        qkv_weight.reshape(model_width, -1),
        preferred_element_type=jnp.float32,
    )
    projected = projected.reshape(prompts, query_count, local_heads, 3 * HEAD)
    queries = rms_norm(projected[..., :HEAD], qk_gains[0]).astype(jnp.bfloat16)
    image_key = rms_norm(projected[..., HEAD : 2 * HEAD], qk_gains[1]).astype(jnp.bfloat16)
    image_value = projected[..., 2 * HEAD :].astype(jnp.bfloat16)
    key_value = jnp.transpose(jnp.concatenate([image_key, image_value], axis=-1), (0, 2, 1, 3))
    all_pairs = lax.all_gather(key_value, "col", axis=2, tiled=True)
    text_count = text_rows.shape[1]
    text_proj = jnp.dot(
        text_rows.reshape(-1, model_width),
        text_kv_weight.reshape(model_width, -1),
        preferred_element_type=jnp.float32,
    )
    text_proj = text_proj.reshape(prompts, text_count, local_heads, 2 * HEAD)
    text_key = jnp.transpose(
        rms_norm(text_proj[..., :HEAD], qk_gains[2]).astype(jnp.bfloat16), (0, 2, 1, 3)
    )
    text_value = jnp.transpose(text_proj[..., HEAD:].astype(jnp.bfloat16), (0, 2, 1, 3))
    text_valid = (positions[None, :] < text_lengths[0][:, None]).astype(jnp.float32)
    score_scale = HEAD ** (-0.5)
    rows_n = lax.axis_size("row")
    row_idx = lax.axis_index("row")
    image_split = image_float.reshape(prompts, rows_n, own_rows, model_width)
    streams = 2 if own_rows % 2 == 0 else 1
    part = own_rows // streams

    def take(x, s):
        return x[:, :, s * part : (s + 1) * part].reshape(prompts, rows_n * part, *x.shape[3:])

    score_scale = HEAD ** (-0.5)
    out_flat = out_weight.reshape(local_heads * HEAD, model_width)

    def attend(head_queries):
        image_weights = jnp.exp(
            jnp.einsum(
                "phqd,phkd->phqk",
                head_queries,
                all_pairs[..., :HEAD],
                preferred_element_type=jnp.float32,
            )
            * score_scale
        )
        text_weights = jnp.exp(
            jnp.einsum(
                "phqd,phkd->phqk", head_queries, text_key, preferred_element_type=jnp.float32
            )
            * score_scale
        )
        text_weights = text_weights * text_valid[:, None, None, :]
        denominator = jnp.sum(image_weights, axis=-1, keepdims=True) + jnp.sum(
            text_weights, axis=-1, keepdims=True
        )
        image_shares = (image_weights / denominator).astype(jnp.bfloat16)
        text_shares = (text_weights / denominator).astype(jnp.bfloat16)
        mixed = jnp.einsum(
            "phqk,phkd->phqd",
            image_shares,
            all_pairs[..., HEAD:],
            preferred_element_type=jnp.float32,
        )
        mixed = mixed + jnp.einsum(
            "phqk,phkd->phqd", text_shares, text_value, preferred_element_type=jnp.float32
        )
        partial_value = jnp.einsum(
            "phqd,hdm->pqm", mixed.astype(jnp.bfloat16), out_weight, preferred_element_type=jnp.float32
        )
        return partial_value.astype(jnp.bfloat16)

    query_split = queries.reshape(prompts, rows_n, own_rows, local_heads, HEAD)
    attentions = []
    piece_value = None
    for s in range(streams):
        head_queries = jnp.transpose(take(query_split, s), (0, 2, 1, 3))
        if piece_value is not None:
            head_queries, piece_value = lax.optimization_barrier((head_queries, piece_value))
            attentions.append(lax.psum(piece_value, "row"))
        next_value = attend(head_queries)
        if attentions:
            next_value, _ = lax.optimization_barrier((next_value, attentions[-1]))
        piece_value = next_value
    attentions.append(lax.psum(piece_value, "row"))
    finals = []
    for s in range(streams):
        mid_rows = take(image_split, s) + modifiers[:, 2] * attentions[s].astype(jnp.float32)
        normed = modulate(mid_rows, modifiers[:, 3], modifiers[:, 4]).astype(jnp.bfloat16)
        hidden_units = jax.nn.gelu(
            jnp.dot(normed.reshape(-1, model_width), up_weight, preferred_element_type=jnp.float32),
            approximate=True,
        ).astype(jnp.bfloat16)
        product = jnp.dot(hidden_units, down_weight, preferred_element_type=jnp.float32)
        product = product.reshape(prompts, rows_n * part, model_width).astype(jnp.bfloat16)
        if s + 1 < streams:
            product, attentions[s + 1] = lax.optimization_barrier((product, attentions[s + 1]))
        if finals:
            product, _ = lax.optimization_barrier((product, finals[-1]))
        feed = lax.psum_scatter(product, "row", scatter_dimension=1, tiled=True).astype(jnp.float32)
        mid_own = lax.dynamic_index_in_dim(
            mid_rows.reshape(prompts, rows_n, part, model_width), row_idx, 1, keepdims=False
        )
        finals.append(mid_own + modifiers[:, 5] * feed)
    final_rows = jnp.concatenate(finals, axis=1)
    final_in = modulate(final_rows, modifiers[:, 8], modifiers[:, 9]).astype(jnp.bfloat16)
    own_velocity = jnp.dot(
        final_in.reshape(-1, model_width), final_weight, preferred_element_type=jnp.float32
    )
    own_velocity = own_velocity.reshape(1, prompts, own_rows, -1)
    both_halves = lax.all_to_all(own_velocity, "cfg", split_axis=3, concat_axis=0, tiled=True)
    conditional = both_halves[0]
    unconditional = both_halves[1]
    velocity = unconditional + guidance[0] * (conditional - unconditional)
    sigma_pair = lax.dynamic_slice_in_dim(sigmas, step_index[0], 2, 0)
    return (velocity, latents + (sigma_pair[1] - sigma_pair[0]) * velocity)


def solution(mesh):
    placed = (
        P("cfg", None, ("row", "col"), None),
        P("cfg", None, "row", None),
        P("cfg", None),
        P("cfg", None, None, None),
        P(),
        P(None, "row", None),
        P(None, "row", None),
        P("row", None, None),
        P(None, "row"),
        P("row", None),
        P(),
        P(None, ("row", "col"), "cfg"),
        P(),
        P(),
        P(),
    )
    return jax.shard_map(
        shards,
        mesh=mesh,
        in_specs=placed,
        out_specs=(P(None, ("row", "col"), "cfg"), P(None, ("row", "col"), "cfg")),
        check_vma=False,
    )
```

```python
import jax
import jax.numpy as jnp
from jax import lax
from jax.sharding import PartitionSpec as P

HEAD = 64


epsilon = 1e-06


def layer_norm(inputs):
    average = jnp.mean(inputs, axis=-1, keepdims=True)
    centered = inputs - average
    variance = jnp.mean(centered * centered, axis=-1, keepdims=True)
    return centered / jnp.sqrt(variance + epsilon)


def modulate(inputs, shifts, scales):
    return layer_norm(inputs) * (1.0 + scales) + shifts


def rms_norm(inputs, norm_gain):
    square_mean = jnp.mean(inputs * inputs, axis=-1, keepdims=True)
    return inputs / jnp.sqrt(square_mean + epsilon) * norm_gain


def line_gather(x, name, axis):
    n = lax.axis_size(name)
    me = lax.axis_index(name)
    blocks = [x]
    sources = [me]
    up = x
    down = x
    for s in range(1, n):
        up = lax.ppermute(up, name, [(k, k + 1) for k in range(n - 1)])
        down = lax.ppermute(down, name, [(k + 1, k) for k in range(n - 1)])
        blocks += [up, down]
        sources += [jnp.where(me - s >= 0, me - s, -1), jnp.where(me + s < n, me + s, -1)]
    return jnp.concatenate(blocks, axis=axis), jnp.stack(sources)


def shards(
    image_tokens,
    text_tokens,
    text_lengths,
    modulation,
    qk_gains,
    qkv_weight,
    text_kv_weight,
    out_weight,
    up_weight,
    down_weight,
    final_weight,
    latents,
    sigmas,
    step_index,
    guidance,
):
    modifiers = modulation[0][:, :, None, :]
    own_image = image_tokens[0]
    prompts = own_image.shape[0]
    own_rows = own_image.shape[1]
    model_width = own_image.shape[2]
    text_own = text_tokens[0].astype(jnp.float32)
    text_in = modulate(text_own, modifiers[:, 6], modifiers[:, 7]).astype(jnp.bfloat16)
    image_rows = lax.all_gather(own_image, "row", axis=1, tiled=True)
    text_local = text_in.shape[1]
    if lax.axis_size("row") <= 4:
        text_rows, sources = line_gather(text_in, "row", 1)
        positions = jnp.where(
            sources[:, None] >= 0,
            sources[:, None] * text_local + jnp.arange(text_local)[None, :],
            jnp.iinfo(jnp.int32).max,
        ).reshape(-1)
    else:
        text_rows = lax.all_gather(text_in, "row", axis=1, tiled=True)
        positions = jnp.arange(text_rows.shape[1])
    query_count = image_rows.shape[1]
    image_float = image_rows.astype(jnp.float32)
    image_in = modulate(image_float, modifiers[:, 0], modifiers[:, 1]).astype(jnp.bfloat16)
    local_heads = qkv_weight.shape[1]
    projected = jnp.dot(
        image_in.reshape(-1, model_width),
        qkv_weight.reshape(model_width, -1),
        preferred_element_type=jnp.float32,
    )
    projected = projected.reshape(prompts, query_count, local_heads, 3 * HEAD)
    queries = rms_norm(projected[..., :HEAD], qk_gains[0]).astype(jnp.bfloat16)
    image_key = rms_norm(projected[..., HEAD : 2 * HEAD], qk_gains[1]).astype(jnp.bfloat16)
    image_value = projected[..., 2 * HEAD :].astype(jnp.bfloat16)
    key_value = jnp.concatenate([image_key, image_value], axis=-1)
    all_pairs = lax.all_gather(key_value, "col", axis=1, tiled=True)
    text_count = text_rows.shape[1]
    text_proj = jnp.dot(
        text_rows.reshape(-1, model_width),
        text_kv_weight.reshape(model_width, -1),
        preferred_element_type=jnp.float32,
    )
    text_proj = text_proj.reshape(prompts, text_count, local_heads, 2 * HEAD)
    text_key = rms_norm(text_proj[..., :HEAD], qk_gains[2]).astype(jnp.bfloat16)
    text_value = text_proj[..., HEAD:].astype(jnp.bfloat16)
    text_valid = (positions[None, :] < text_lengths[0][:, None]).astype(jnp.float32)
    score_scale = HEAD ** (-0.5)
    rows_n = lax.axis_size("row")
    row_idx = lax.axis_index("row")
    image_split = image_float.reshape(prompts, rows_n, own_rows, model_width)
    first = own_rows // 4 if own_rows % 4 == 0 else own_rows
    bounds = [0, first, own_rows] if first < own_rows else [0, own_rows]
    streams = len(bounds) - 1

    def take(x, s):
        count = bounds[s + 1] - bounds[s]
        return x[:, :, bounds[s] : bounds[s + 1]].reshape(prompts, rows_n * count, *x.shape[3:])

    score_scale = HEAD ** (-0.5)
    out_flat = out_weight.reshape(local_heads * HEAD, model_width)

    def attend(head_queries):
        image_weights = jnp.exp(
            jnp.einsum(
                "pqhd,pkhd->phqk",
                head_queries,
                all_pairs[..., :HEAD],
                preferred_element_type=jnp.float32,
            )
            * score_scale
        )
        text_weights = jnp.exp(
            jnp.einsum(
                "pqhd,pkhd->phqk", head_queries, text_key, preferred_element_type=jnp.float32
            )
            * score_scale
        )
        text_weights = text_weights * text_valid[:, None, None, :]
        denominator = jnp.sum(image_weights, axis=-1, keepdims=True) + jnp.sum(
            text_weights, axis=-1, keepdims=True
        )
        image_shares = (image_weights / denominator).astype(jnp.bfloat16)
        text_shares = (text_weights / denominator).astype(jnp.bfloat16)
        mixed = jnp.einsum(
            "phqk,pkhd->pqhd",
            image_shares,
            all_pairs[..., HEAD:],
            preferred_element_type=jnp.float32,
        )
        mixed = mixed + jnp.einsum(
            "phqk,pkhd->pqhd", text_shares, text_value, preferred_element_type=jnp.float32
        )
        count = head_queries.shape[1]
        head_rows = mixed.astype(jnp.bfloat16).reshape(prompts * count, local_heads * HEAD)
        partial_value = jnp.dot(head_rows, out_flat, preferred_element_type=jnp.float32)
        return partial_value.reshape(prompts, count, model_width).astype(jnp.bfloat16)

    query_split = queries.reshape(prompts, rows_n, own_rows, local_heads, HEAD)
    attentions = []
    piece_value = None
    for s in range(streams):
        head_queries = take(query_split, s)
        if piece_value is not None:
            head_queries, piece_value = lax.optimization_barrier((head_queries, piece_value))
            attentions.append(lax.psum(piece_value, "row"))
        next_value = attend(head_queries)
        if attentions:
            next_value, _ = lax.optimization_barrier((next_value, attentions[-1]))
        piece_value = next_value
    attentions.append(lax.psum(piece_value, "row"))
    finals = []
    for s in range(streams):
        mid_rows = take(image_split, s) + modifiers[:, 2] * attentions[s].astype(jnp.float32)
        normed = modulate(mid_rows, modifiers[:, 3], modifiers[:, 4]).astype(jnp.bfloat16)
        hidden_units = jax.nn.gelu(
            jnp.dot(normed.reshape(-1, model_width), up_weight, preferred_element_type=jnp.float32),
            approximate=True,
        ).astype(jnp.bfloat16)
        product = jnp.dot(hidden_units, down_weight, preferred_element_type=jnp.float32)
        product = product.reshape(prompts, -1, model_width).astype(jnp.bfloat16)
        if s + 1 < streams:
            product, attentions[s + 1] = lax.optimization_barrier((product, attentions[s + 1]))
        if finals:
            product, _ = lax.optimization_barrier((product, finals[-1]))
        feed = lax.psum_scatter(product, "row", scatter_dimension=1, tiled=True).astype(jnp.float32)
        mid_own = lax.dynamic_index_in_dim(
            mid_rows.reshape(prompts, rows_n, -1, model_width), row_idx, 1, keepdims=False
        )
        finals.append(mid_own + modifiers[:, 5] * feed)
    final_rows = jnp.concatenate(finals, axis=1)
    final_in = modulate(final_rows, modifiers[:, 8], modifiers[:, 9]).astype(jnp.bfloat16)
    own_velocity = jnp.dot(
        final_in.reshape(-1, model_width), final_weight, preferred_element_type=jnp.float32
    )
    own_velocity = own_velocity.reshape(1, prompts, own_rows, -1)
    both_halves = lax.all_to_all(own_velocity, "cfg", split_axis=3, concat_axis=0, tiled=True)
    conditional = both_halves[0]
    unconditional = both_halves[1]
    velocity = unconditional + guidance[0] * (conditional - unconditional)
    sigma_pair = lax.dynamic_slice_in_dim(sigmas, step_index[0], 2, 0)
    return (velocity, latents + (sigma_pair[1] - sigma_pair[0]) * velocity)


def solution(mesh):
    placed = (
        P("cfg", None, ("row", "col"), None),
        P("cfg", None, "row", None),
        P("cfg", None),
        P("cfg", None, None, None),
        P(),
        P(None, "row", None),
        P(None, "row", None),
        P("row", None, None),
        P(None, "row"),
        P("row", None),
        P(),
        P(None, ("row", "col"), "cfg"),
        P(),
        P(),
        P(),
    )
    return jax.shard_map(
        shards,
        mesh=mesh,
        in_specs=placed,
        out_specs=(P(None, ("row", "col"), "cfg"), P(None, ("row", "col"), "cfg")),
        check_vma=False,
    )
```

```python
import jax
import jax.numpy as jnp
from jax import lax
from jax.sharding import PartitionSpec as P

HEAD = 64


epsilon = 1e-06


def layer_norm(inputs):
    average = jnp.mean(inputs, axis=-1, keepdims=True)
    centered = inputs - average
    variance = jnp.mean(centered * centered, axis=-1, keepdims=True)
    return centered / jnp.sqrt(variance + epsilon)


def modulate(inputs, shifts, scales):
    return layer_norm(inputs) * (1.0 + scales) + shifts


def rms_norm(inputs, norm_gain):
    square_mean = jnp.mean(inputs * inputs, axis=-1, keepdims=True)
    return inputs / jnp.sqrt(square_mean + epsilon) * norm_gain


def line_gather(x, name, axis):
    n = lax.axis_size(name)
    me = lax.axis_index(name)
    blocks = [x]
    sources = [me]
    up = x
    down = x
    for s in range(1, n):
        up = lax.ppermute(up, name, [(k, k + 1) for k in range(n - 1)])
        down = lax.ppermute(down, name, [(k + 1, k) for k in range(n - 1)])
        blocks += [up, down]
        sources += [jnp.where(me - s >= 0, me - s, -1), jnp.where(me + s < n, me + s, -1)]
    return jnp.concatenate(blocks, axis=axis), jnp.stack(sources)


def shards(
    image_tokens,
    text_tokens,
    text_lengths,
    modulation,
    qk_gains,
    qkv_weight,
    text_kv_weight,
    out_weight,
    up_weight,
    down_weight,
    final_weight,
    latents,
    sigmas,
    step_index,
    guidance,
):
    modifiers = modulation[0][:, :, None, :]
    own_image = image_tokens[0]
    prompts = own_image.shape[0]
    own_rows = own_image.shape[1]
    model_width = own_image.shape[2]
    text_own = text_tokens[0].astype(jnp.float32)
    text_in = modulate(text_own, modifiers[:, 6], modifiers[:, 7]).astype(jnp.bfloat16)
    image_rows = lax.all_gather(own_image, "row", axis=1, tiled=True)
    text_local = text_in.shape[1]
    if lax.axis_size("row") <= 4:
        text_rows, sources = line_gather(text_in, "row", 1)
        positions = jnp.where(
            sources[:, None] >= 0,
            sources[:, None] * text_local + jnp.arange(text_local)[None, :],
            jnp.iinfo(jnp.int32).max,
        ).reshape(-1)
    else:
        text_rows = lax.all_gather(text_in, "row", axis=1, tiled=True)
        positions = jnp.arange(text_rows.shape[1])
    query_count = image_rows.shape[1]
    image_float = image_rows.astype(jnp.float32)
    image_in = modulate(image_float, modifiers[:, 0], modifiers[:, 1]).astype(jnp.bfloat16)
    local_heads = qkv_weight.shape[1]
    projected = jnp.dot(
        image_in.reshape(-1, model_width),
        qkv_weight.reshape(model_width, -1),
        preferred_element_type=jnp.float32,
    )
    projected = projected.reshape(prompts, query_count, local_heads, 3 * HEAD)
    queries = rms_norm(projected[..., :HEAD], qk_gains[0]).astype(jnp.bfloat16)
    image_key = rms_norm(projected[..., HEAD : 2 * HEAD], qk_gains[1]).astype(jnp.bfloat16)
    image_value = projected[..., 2 * HEAD :].astype(jnp.bfloat16)
    key_value = jnp.concatenate([image_key, image_value], axis=-1)
    all_pairs = lax.all_gather(key_value, "col", axis=1, tiled=True)
    text_count = text_rows.shape[1]
    text_proj = jnp.dot(
        text_rows.reshape(-1, model_width),
        text_kv_weight.reshape(model_width, -1),
        preferred_element_type=jnp.float32,
    )
    text_proj = text_proj.reshape(prompts, text_count, local_heads, 2 * HEAD)
    text_key = rms_norm(text_proj[..., :HEAD], qk_gains[2]).astype(jnp.bfloat16)
    text_value = text_proj[..., HEAD:].astype(jnp.bfloat16)
    text_valid = (positions[None, :] < text_lengths[0][:, None]).astype(jnp.float32)
    score_scale = HEAD ** (-0.5)
    image_weights = jnp.exp(
        jnp.einsum(
            "pqhd,pkhd->phqk", queries, all_pairs[..., :HEAD], preferred_element_type=jnp.float32
        )
        * score_scale
    )
    text_weights = jnp.exp(
        jnp.einsum("pqhd,pkhd->phqk", queries, text_key, preferred_element_type=jnp.float32)
        * score_scale
    )
    text_weights = text_weights * text_valid[:, None, None, :]
    denominator = jnp.sum(image_weights, axis=-1, keepdims=True) + jnp.sum(
        text_weights, axis=-1, keepdims=True
    )
    inverse = 1.0 / denominator
    image_shares = (image_weights * inverse).astype(jnp.bfloat16)
    text_shares = (text_weights * inverse).astype(jnp.bfloat16)
    mixed = jnp.einsum(
        "phqk,pkhd->pqhd", image_shares, all_pairs[..., HEAD:], preferred_element_type=jnp.float32
    )
    mixed = mixed + jnp.einsum(
        "phqk,pkhd->pqhd", text_shares, text_value, preferred_element_type=jnp.float32
    )
    head_rows = mixed.astype(jnp.bfloat16).reshape(prompts * query_count, local_heads * HEAD)
    out_flat = out_weight.reshape(local_heads * HEAD, model_width)
    partial_value = jnp.dot(head_rows, out_flat, preferred_element_type=jnp.float32)
    rows_n = lax.axis_size("row")
    row_idx = lax.axis_index("row")
    partial_value = partial_value.astype(jnp.bfloat16).reshape(prompts, rows_n, own_rows, model_width)
    image_split = image_float.reshape(prompts, rows_n, own_rows, model_width)
    streams = 2 if own_rows % 2 == 0 else 1
    part = own_rows // streams

    def take(x, s):
        return x[:, :, s * part : (s + 1) * part].reshape(prompts, rows_n * part, model_width)

    attentions = []
    for s in range(streams):
        piece_value = take(partial_value, s)
        if attentions:
            piece_value, _ = lax.optimization_barrier((piece_value, attentions[-1]))
        attentions.append(lax.psum(piece_value, "row"))
    finals = []
    for s in range(streams):
        mid_rows = take(image_split, s) + modifiers[:, 2] * attentions[s].astype(jnp.float32)
        normed = modulate(mid_rows, modifiers[:, 3], modifiers[:, 4]).astype(jnp.bfloat16)
        hidden_units = jax.nn.gelu(
            jnp.dot(normed.reshape(-1, model_width), up_weight, preferred_element_type=jnp.float32),
            approximate=True,
        ).astype(jnp.bfloat16)
        product = jnp.dot(hidden_units, down_weight, preferred_element_type=jnp.float32)
        product = product.reshape(prompts, rows_n * part, model_width).astype(jnp.bfloat16)
        if s + 1 < streams:
            product, attentions[s + 1] = lax.optimization_barrier((product, attentions[s + 1]))
        feed = lax.psum_scatter(product, "row", scatter_dimension=1, tiled=True).astype(jnp.float32)
        mid_own = lax.dynamic_index_in_dim(
            mid_rows.reshape(prompts, rows_n, part, model_width), row_idx, 1, keepdims=False
        )
        finals.append(mid_own + modifiers[:, 5] * feed)
    final_rows = jnp.concatenate(finals, axis=1)
    final_in = modulate(final_rows, modifiers[:, 8], modifiers[:, 9]).astype(jnp.bfloat16)
    own_velocity = jnp.dot(
        final_in.reshape(-1, model_width), final_weight, preferred_element_type=jnp.float32
    )
    own_velocity = own_velocity.reshape(1, prompts, own_rows, -1)
    both_halves = lax.all_to_all(own_velocity, "cfg", split_axis=3, concat_axis=0, tiled=True)
    conditional = both_halves[0]
    unconditional = both_halves[1]
    velocity = unconditional + guidance[0] * (conditional - unconditional)
    sigma_pair = lax.dynamic_slice_in_dim(sigmas, step_index[0], 2, 0)
    return (velocity, latents + (sigma_pair[1] - sigma_pair[0]) * velocity)


def solution(mesh):
    placed = (
        P("cfg", None, ("row", "col"), None),
        P("cfg", None, "row", None),
        P("cfg", None),
        P("cfg", None, None, None),
        P(),
        P(None, "row", None),
        P(None, "row", None),
        P("row", None, None),
        P(None, "row"),
        P("row", None),
        P(),
        P(None, ("row", "col"), "cfg"),
        P(),
        P(),
        P(),
    )
    return jax.shard_map(
        shards,
        mesh=mesh,
        in_specs=placed,
        out_specs=(P(None, ("row", "col"), "cfg"), P(None, ("row", "col"), "cfg")),
        check_vma=False,
    )
```

```python
import jax
import jax.numpy as jnp
from jax import lax
from jax.sharding import PartitionSpec as P

HEAD = 64


epsilon = 1e-06


def layer_norm(inputs):
    average = jnp.mean(inputs, axis=-1, keepdims=True)
    centered = inputs - average
    variance = jnp.mean(centered * centered, axis=-1, keepdims=True)
    return centered / jnp.sqrt(variance + epsilon)


def modulate(inputs, shifts, scales):
    return layer_norm(inputs) * (1.0 + scales) + shifts


def rms_norm(inputs, norm_gain):
    square_mean = jnp.mean(inputs * inputs, axis=-1, keepdims=True)
    return inputs / jnp.sqrt(square_mean + epsilon) * norm_gain


def line_gather(x, name, axis):
    n = lax.axis_size(name)
    me = lax.axis_index(name)
    blocks = [x]
    sources = [me]
    up = x
    down = x
    for s in range(1, n):
        up = lax.ppermute(up, name, [(k, k + 1) for k in range(n - 1)])
        down = lax.ppermute(down, name, [(k + 1, k) for k in range(n - 1)])
        blocks += [up, down]
        sources += [jnp.where(me - s >= 0, me - s, -1), jnp.where(me + s < n, me + s, -1)]
    return jnp.concatenate(blocks, axis=axis), jnp.stack(sources)


def shards(
    image_tokens,
    text_tokens,
    text_lengths,
    modulation,
    qk_gains,
    qkv_weight,
    text_kv_weight,
    out_weight,
    up_weight,
    down_weight,
    final_weight,
    latents,
    sigmas,
    step_index,
    guidance,
):
    modifiers = modulation[0][:, :, None, :]
    own_image = image_tokens[0]
    prompts = own_image.shape[0]
    own_rows = own_image.shape[1]
    model_width = own_image.shape[2]
    text_own = text_tokens[0].astype(jnp.float32)
    text_in = modulate(text_own, modifiers[:, 6], modifiers[:, 7]).astype(jnp.bfloat16)
    image_rows = lax.all_gather(own_image, "row", axis=1, tiled=True)
    text_local = text_in.shape[1]
    if lax.axis_size("row") <= 4:
        text_rows, sources = line_gather(text_in, "row", 1)
        positions = jnp.where(
            sources[:, None] >= 0,
            sources[:, None] * text_local + jnp.arange(text_local)[None, :],
            jnp.iinfo(jnp.int32).max,
        ).reshape(-1)
    else:
        text_rows = lax.all_gather(text_in, "row", axis=1, tiled=True)
        positions = jnp.arange(text_rows.shape[1])
    query_count = image_rows.shape[1]
    image_float = image_rows.astype(jnp.float32)
    image_in = modulate(image_float, modifiers[:, 0], modifiers[:, 1]).astype(jnp.bfloat16)
    local_heads = qkv_weight.shape[1]
    projected = jnp.dot(
        image_in.reshape(-1, model_width),
        qkv_weight.reshape(model_width, -1),
        preferred_element_type=jnp.float32,
    )
    projected = projected.reshape(prompts, query_count, local_heads, 3 * HEAD)
    queries = rms_norm(projected[..., :HEAD], qk_gains[0]).astype(jnp.bfloat16)
    image_key = rms_norm(projected[..., HEAD : 2 * HEAD], qk_gains[1]).astype(jnp.bfloat16)
    image_value = projected[..., 2 * HEAD :].astype(jnp.bfloat16)
    key_value = jnp.concatenate([image_key, image_value], axis=-1)
    all_pairs = lax.all_gather(key_value, "col", axis=1, tiled=True)
    text_count = text_rows.shape[1]
    text_proj = jnp.dot(
        text_rows.reshape(-1, model_width),
        text_kv_weight.reshape(model_width, -1),
        preferred_element_type=jnp.float32,
    )
    text_proj = text_proj.reshape(prompts, text_count, local_heads, 2 * HEAD)
    text_key = rms_norm(text_proj[..., :HEAD], qk_gains[2]).astype(jnp.bfloat16)
    text_value = text_proj[..., HEAD:].astype(jnp.bfloat16)
    text_valid = (positions[None, :] < text_lengths[0][:, None]).astype(jnp.float32)
    score_scale = HEAD ** (-0.5)
    image_weights = jnp.exp(
        jnp.einsum(
            "pqhd,pkhd->phqk", queries, all_pairs[..., :HEAD], preferred_element_type=jnp.float32
        )
        * score_scale
    )
    text_weights = jnp.exp(
        jnp.einsum("pqhd,pkhd->phqk", queries, text_key, preferred_element_type=jnp.float32)
        * score_scale
    )
    text_weights = text_weights * text_valid[:, None, None, :]
    denominator = jnp.sum(image_weights, axis=-1, keepdims=True) + jnp.sum(
        text_weights, axis=-1, keepdims=True
    )
    inverse = 1.0 / denominator
    image_shares = (image_weights * inverse).astype(jnp.bfloat16)
    text_shares = (text_weights * inverse).astype(jnp.bfloat16)
    mixed = jnp.einsum(
        "phqk,pkhd->pqhd", image_shares, all_pairs[..., HEAD:], preferred_element_type=jnp.float32
    )
    mixed = mixed + jnp.einsum(
        "phqk,pkhd->pqhd", text_shares, text_value, preferred_element_type=jnp.float32
    )
    head_rows = mixed.astype(jnp.bfloat16).reshape(prompts * query_count, local_heads * HEAD)
    out_flat = out_weight.reshape(local_heads * HEAD, model_width)
    partial_value = jnp.dot(head_rows, out_flat, preferred_element_type=jnp.float32)
    rows_n = lax.axis_size("row")
    row_idx = lax.axis_index("row")
    partial_value = partial_value.astype(jnp.bfloat16).reshape(prompts, rows_n, own_rows, model_width)
    image_split = image_float.reshape(prompts, rows_n, own_rows, model_width)
    streams = 2 if own_rows % 2 == 0 else 1
    part = own_rows // streams

    def take(x, s):
        return x[:, :, s * part : (s + 1) * part].reshape(prompts, rows_n * part, model_width)

    attentions = []
    for s in range(streams):
        piece_value = take(partial_value, s)
        if attentions:
            piece_value, _ = lax.optimization_barrier((piece_value, attentions[-1]))
        attentions.append(lax.psum(piece_value, "row"))
    finals = []
    for s in range(streams):
        mid_rows = take(image_split, s) + modifiers[:, 2] * attentions[s].astype(jnp.float32)
        normed = modulate(mid_rows, modifiers[:, 3], modifiers[:, 4]).astype(jnp.bfloat16)
        hidden_units = jax.nn.gelu(
            jnp.dot(normed.reshape(-1, model_width), up_weight, preferred_element_type=jnp.float32),
            approximate=True,
        ).astype(jnp.bfloat16)
        product = jnp.dot(hidden_units, down_weight, preferred_element_type=jnp.float32)
        product = product.reshape(prompts, rows_n * part, model_width).astype(jnp.bfloat16)
        if s + 1 < streams:
            product, attentions[s + 1] = lax.optimization_barrier((product, attentions[s + 1]))
        if finals:
            product, _ = lax.optimization_barrier((product, finals[-1]))
        feed = lax.psum_scatter(product, "row", scatter_dimension=1, tiled=True).astype(jnp.float32)
        mid_own = lax.dynamic_index_in_dim(
            mid_rows.reshape(prompts, rows_n, part, model_width), row_idx, 1, keepdims=False
        )
        finals.append(mid_own + modifiers[:, 5] * feed)
    final_rows = jnp.concatenate(finals, axis=1)
    final_in = modulate(final_rows, modifiers[:, 8], modifiers[:, 9]).astype(jnp.bfloat16)
    own_velocity = jnp.dot(
        final_in.reshape(-1, model_width), final_weight, preferred_element_type=jnp.float32
    )
    own_velocity = own_velocity.reshape(1, prompts, own_rows, -1)
    both_halves = lax.all_to_all(own_velocity, "cfg", split_axis=3, concat_axis=0, tiled=True)
    conditional = both_halves[0]
    unconditional = both_halves[1]
    velocity = unconditional + guidance[0] * (conditional - unconditional)
    sigma_pair = lax.dynamic_slice_in_dim(sigmas, step_index[0], 2, 0)
    return (velocity, latents + (sigma_pair[1] - sigma_pair[0]) * velocity)


def solution(mesh):
    placed = (
        P("cfg", None, ("row", "col"), None),
        P("cfg", None, "row", None),
        P("cfg", None),
        P("cfg", None, None, None),
        P(),
        P(None, "row", None),
        P(None, "row", None),
        P("row", None, None),
        P(None, "row"),
        P("row", None),
        P(),
        P(None, ("row", "col"), "cfg"),
        P(),
        P(),
        P(),
    )
    return jax.shard_map(
        shards,
        mesh=mesh,
        in_specs=placed,
        out_specs=(P(None, ("row", "col"), "cfg"), P(None, ("row", "col"), "cfg")),
        check_vma=False,
    )
```

```python
import jax
import jax.numpy as jnp
from jax import lax
from jax.sharding import PartitionSpec as P

HEAD = 64


epsilon = 1e-06


def layer_norm(inputs):
    average = jnp.mean(inputs, axis=-1, keepdims=True)
    centered = inputs - average
    variance = jnp.mean(centered * centered, axis=-1, keepdims=True)
    return centered / jnp.sqrt(variance + epsilon)


def modulate(inputs, shifts, scales):
    return layer_norm(inputs) * (1.0 + scales) + shifts


def rms_norm(inputs, norm_gain):
    square_mean = jnp.mean(inputs * inputs, axis=-1, keepdims=True)
    return inputs / jnp.sqrt(square_mean + epsilon) * norm_gain


def line_gather(x, name, axis):
    n = lax.axis_size(name)
    me = lax.axis_index(name)
    blocks = [x]
    sources = [me]
    up = x
    down = x
    for s in range(1, n):
        up = lax.ppermute(up, name, [(k, k + 1) for k in range(n - 1)])
        down = lax.ppermute(down, name, [(k + 1, k) for k in range(n - 1)])
        blocks += [up, down]
        sources += [jnp.where(me - s >= 0, me - s, -1), jnp.where(me + s < n, me + s, -1)]
    return jnp.concatenate(blocks, axis=axis), jnp.stack(sources)


def shards(
    image_tokens,
    text_tokens,
    text_lengths,
    modulation,
    qk_gains,
    qkv_weight,
    text_kv_weight,
    out_weight,
    up_weight,
    down_weight,
    final_weight,
    latents,
    sigmas,
    step_index,
    guidance,
):
    modifiers = modulation[0][:, :, None, :]
    own_image = image_tokens[0]
    prompts = own_image.shape[0]
    own_rows = own_image.shape[1]
    model_width = own_image.shape[2]
    text_own = text_tokens[0].astype(jnp.float32)
    text_in = modulate(text_own, modifiers[:, 6], modifiers[:, 7]).astype(jnp.bfloat16)
    image_rows = lax.all_gather(own_image, "row", axis=1, tiled=True)
    text_local = text_in.shape[1]
    if lax.axis_size("row") <= 4:
        text_rows, sources = line_gather(text_in, "row", 1)
        positions = jnp.where(
            sources[:, None] >= 0,
            sources[:, None] * text_local + jnp.arange(text_local)[None, :],
            jnp.iinfo(jnp.int32).max,
        ).reshape(-1)
    else:
        text_rows = lax.all_gather(text_in, "row", axis=1, tiled=True)
        positions = jnp.arange(text_rows.shape[1])
    query_count = image_rows.shape[1]
    image_float = image_rows.astype(jnp.float32)
    image_in = modulate(image_float, modifiers[:, 0], modifiers[:, 1]).astype(jnp.bfloat16)
    local_heads = qkv_weight.shape[1]
    projected = jnp.dot(
        image_in.reshape(-1, model_width),
        qkv_weight.reshape(model_width, -1),
        preferred_element_type=jnp.float32,
    )
    projected = projected.reshape(prompts, query_count, local_heads, 3 * HEAD)
    queries = rms_norm(projected[..., :HEAD], qk_gains[0]).astype(jnp.bfloat16)
    image_key = rms_norm(projected[..., HEAD : 2 * HEAD], qk_gains[1]).astype(jnp.bfloat16)
    image_value = projected[..., 2 * HEAD :].astype(jnp.bfloat16)
    key_value = jnp.concatenate([image_key, image_value], axis=-1)
    all_pairs = lax.all_gather(key_value, "col", axis=1, tiled=True)
    text_count = text_rows.shape[1]
    text_proj = jnp.dot(
        text_rows.reshape(-1, model_width),
        text_kv_weight.reshape(model_width, -1),
        preferred_element_type=jnp.float32,
    )
    text_proj = text_proj.reshape(prompts, text_count, local_heads, 2 * HEAD)
    text_key = rms_norm(text_proj[..., :HEAD], qk_gains[2]).astype(jnp.bfloat16)
    text_value = text_proj[..., HEAD:].astype(jnp.bfloat16)
    text_valid = (positions[None, :] < text_lengths[0][:, None]).astype(jnp.float32)
    score_scale = HEAD ** (-0.5)
    image_weights = jnp.exp(
        jnp.einsum(
            "pqhd,pkhd->phqk", queries, all_pairs[..., :HEAD], preferred_element_type=jnp.float32
        )
        * score_scale
    )
    text_weights = jnp.exp(
        jnp.einsum("pqhd,pkhd->phqk", queries, text_key, preferred_element_type=jnp.float32)
        * score_scale
    )
    text_weights = text_weights * text_valid[:, None, None, :]
    denominator = jnp.sum(image_weights, axis=-1, keepdims=True) + jnp.sum(
        text_weights, axis=-1, keepdims=True
    )
    image_shares = (image_weights / denominator).astype(jnp.bfloat16)
    text_shares = (text_weights / denominator).astype(jnp.bfloat16)
    mixed = jnp.einsum(
        "phqk,pkhd->pqhd", image_shares, all_pairs[..., HEAD:], preferred_element_type=jnp.float32
    )
    mixed = mixed + jnp.einsum(
        "phqk,pkhd->pqhd", text_shares, text_value, preferred_element_type=jnp.float32
    )
    head_rows = mixed.astype(jnp.bfloat16).reshape(prompts * query_count, local_heads * HEAD)
    out_flat = out_weight.reshape(local_heads * HEAD, model_width)
    partial_value = jnp.dot(head_rows, out_flat, preferred_element_type=jnp.float32)
    rows_n = lax.axis_size("row")
    row_idx = lax.axis_index("row")
    partial_value = partial_value.astype(jnp.bfloat16).reshape(prompts, rows_n, own_rows, model_width)
    image_split = image_float.reshape(prompts, rows_n, own_rows, model_width)
    streams = 2 if own_rows % 2 == 0 else 1
    part = own_rows // streams

    def take(x, s):
        return x[:, :, s * part : (s + 1) * part].reshape(prompts, rows_n * part, model_width)

    attentions = []
    for s in range(streams):
        piece_value = take(partial_value, s)
        if attentions:
            piece_value, _ = lax.optimization_barrier((piece_value, attentions[-1]))
        attentions.append(lax.psum(piece_value, "row"))
    finals = []
    for s in range(streams):
        mid_rows = take(image_split, s) + modifiers[:, 2] * attentions[s].astype(jnp.float32)
        normed = modulate(mid_rows, modifiers[:, 3], modifiers[:, 4]).astype(jnp.bfloat16)
        hidden_units = jax.nn.gelu(
            jnp.dot(normed.reshape(-1, model_width), up_weight, preferred_element_type=jnp.float32),
            approximate=True,
        ).astype(jnp.bfloat16)
        product = jnp.dot(hidden_units, down_weight, preferred_element_type=jnp.float32)
        product = product.reshape(prompts, rows_n * part, model_width).astype(jnp.bfloat16)
        if s + 1 < streams:
            product, attentions[s + 1] = lax.optimization_barrier((product, attentions[s + 1]))
        feed = lax.psum_scatter(product, "row", scatter_dimension=1, tiled=True).astype(jnp.float32)
        mid_own = lax.dynamic_index_in_dim(
            mid_rows.reshape(prompts, rows_n, part, model_width), row_idx, 1, keepdims=False
        )
        finals.append(mid_own + modifiers[:, 5] * feed)
    final_rows = jnp.concatenate(finals, axis=1)
    final_in = modulate(final_rows, modifiers[:, 8], modifiers[:, 9]).astype(jnp.bfloat16)
    own_velocity = jnp.dot(
        final_in.reshape(-1, model_width), final_weight, preferred_element_type=jnp.float32
    )
    own_velocity = own_velocity.reshape(1, prompts, own_rows, -1)
    half = lax.axis_index("cfg")
    width = own_velocity.shape[-1] // 2
    mine = lax.dynamic_slice_in_dim(own_velocity[0], half * width, width, 2)
    wanted = lax.dynamic_slice_in_dim(own_velocity[0], (1 - half) * width, width, 2)
    received = lax.ppermute(wanted, "cfg", [(0, 1), (1, 0)])
    conditional = jnp.where(half == 0, mine, received)
    unconditional = jnp.where(half == 0, received, mine)
    velocity = unconditional + guidance[0] * (conditional - unconditional)
    sigma_pair = lax.dynamic_slice_in_dim(sigmas, step_index[0], 2, 0)
    return (velocity, latents + (sigma_pair[1] - sigma_pair[0]) * velocity)


def solution(mesh):
    placed = (
        P("cfg", None, ("row", "col"), None),
        P("cfg", None, "row", None),
        P("cfg", None),
        P("cfg", None, None, None),
        P(),
        P(None, "row", None),
        P(None, "row", None),
        P("row", None, None),
        P(None, "row"),
        P("row", None),
        P(),
        P(None, ("row", "col"), "cfg"),
        P(),
        P(),
        P(),
    )
    return jax.shard_map(
        shards,
        mesh=mesh,
        in_specs=placed,
        out_specs=(P(None, ("row", "col"), "cfg"), P(None, ("row", "col"), "cfg")),
        check_vma=False,
    )
```

```python
import jax
import jax.numpy as jnp
from jax import lax
from jax.sharding import PartitionSpec as P

HEAD = 64


epsilon = 1e-06


def layer_norm(inputs):
    average = jnp.mean(inputs, axis=-1, keepdims=True)
    centered = inputs - average
    variance = jnp.mean(centered * centered, axis=-1, keepdims=True)
    return centered / jnp.sqrt(variance + epsilon)


def modulate(inputs, shifts, scales):
    return layer_norm(inputs) * (1.0 + scales) + shifts


def rms_norm(inputs, norm_gain):
    square_mean = jnp.mean(inputs * inputs, axis=-1, keepdims=True)
    return inputs / jnp.sqrt(square_mean + epsilon) * norm_gain


def line_gather(x, name, axis):
    n = lax.axis_size(name)
    me = lax.axis_index(name)
    blocks = [x]
    sources = [me]
    up = x
    down = x
    for s in range(1, n):
        up = lax.ppermute(up, name, [(k, k + 1) for k in range(n - 1)])
        down = lax.ppermute(down, name, [(k + 1, k) for k in range(n - 1)])
        blocks += [up, down]
        sources += [jnp.where(me - s >= 0, me - s, -1), jnp.where(me + s < n, me + s, -1)]
    return jnp.concatenate(blocks, axis=axis), jnp.stack(sources)


def shards(
    image_tokens,
    text_tokens,
    text_lengths,
    modulation,
    qk_gains,
    qkv_weight,
    text_kv_weight,
    out_weight,
    up_weight,
    down_weight,
    final_weight,
    latents,
    sigmas,
    step_index,
    guidance,
):
    modifiers = modulation[0][:, :, None, :]
    own_image = image_tokens[0]
    prompts = own_image.shape[0]
    own_rows = own_image.shape[1]
    model_width = own_image.shape[2]
    text_own = text_tokens[0].astype(jnp.float32)
    text_in = modulate(text_own, modifiers[:, 6], modifiers[:, 7]).astype(jnp.bfloat16)
    image_rows = lax.all_gather(own_image, "row", axis=1, tiled=True)
    text_local = text_in.shape[1]
    if lax.axis_size("row") <= 4:
        text_rows, sources = line_gather(text_in, "row", 1)
        positions = jnp.where(
            sources[:, None] >= 0,
            sources[:, None] * text_local + jnp.arange(text_local)[None, :],
            jnp.iinfo(jnp.int32).max,
        ).reshape(-1)
    else:
        text_rows = lax.all_gather(text_in, "row", axis=1, tiled=True)
        positions = jnp.arange(text_rows.shape[1])
    query_count = image_rows.shape[1]
    image_float = image_rows.astype(jnp.float32)
    image_in = modulate(image_float, modifiers[:, 0], modifiers[:, 1]).astype(jnp.bfloat16)
    local_heads = qkv_weight.shape[1]
    projected = jnp.dot(
        image_in.reshape(-1, model_width),
        qkv_weight.reshape(model_width, -1),
        preferred_element_type=jnp.float32,
    )
    projected = projected.reshape(prompts, query_count, local_heads, 3 * HEAD)
    queries = rms_norm(projected[..., :HEAD], qk_gains[0]).astype(jnp.bfloat16)
    image_key = rms_norm(projected[..., HEAD : 2 * HEAD], qk_gains[1]).astype(jnp.bfloat16)
    image_value = projected[..., 2 * HEAD :].astype(jnp.bfloat16)
    key_value = jnp.concatenate([image_key, image_value], axis=-1)
    all_pairs = lax.all_gather(key_value, "col", axis=1, tiled=True)
    text_count = text_rows.shape[1]
    text_proj = jnp.einsum(
        "ptm,mhe->pthe", text_rows, text_kv_weight, preferred_element_type=jnp.float32
    )
    text_key = rms_norm(text_proj[..., :HEAD], qk_gains[2]).astype(jnp.bfloat16)
    text_value = text_proj[..., HEAD:].astype(jnp.bfloat16)
    text_valid = (positions[None, :] < text_lengths[0][:, None]).astype(jnp.float32)
    score_scale = HEAD ** (-0.5)
    image_weights = jnp.exp(
        jnp.einsum(
            "pqhd,pkhd->phqk", queries, all_pairs[..., :HEAD], preferred_element_type=jnp.float32
        )
        * score_scale
    )
    text_weights = jnp.exp(
        jnp.einsum("pqhd,pkhd->phqk", queries, text_key, preferred_element_type=jnp.float32)
        * score_scale
    )
    text_weights = text_weights * text_valid[:, None, None, :]
    denominator = jnp.sum(image_weights, axis=-1, keepdims=True) + jnp.sum(
        text_weights, axis=-1, keepdims=True
    )
    image_shares = (image_weights / denominator).astype(jnp.bfloat16)
    text_shares = (text_weights / denominator).astype(jnp.bfloat16)
    mixed = jnp.einsum(
        "phqk,pkhd->pqhd", image_shares, all_pairs[..., HEAD:], preferred_element_type=jnp.float32
    )
    mixed = mixed + jnp.einsum(
        "phqk,pkhd->pqhd", text_shares, text_value, preferred_element_type=jnp.float32
    )
    head_rows = mixed.astype(jnp.bfloat16).reshape(prompts * query_count, local_heads * HEAD)
    out_flat = out_weight.reshape(local_heads * HEAD, model_width)
    partial_value = jnp.dot(head_rows, out_flat, preferred_element_type=jnp.float32)
    rows_n = lax.axis_size("row")
    row_idx = lax.axis_index("row")
    partial_value = partial_value.astype(jnp.bfloat16).reshape(prompts, rows_n, own_rows, model_width)
    image_split = image_float.reshape(prompts, rows_n, own_rows, model_width)
    streams = 2 if own_rows % 2 == 0 else 1
    part = own_rows // streams

    def take(x, s):
        return x[:, :, s * part : (s + 1) * part].reshape(prompts, rows_n * part, model_width)

    attentions = []
    for s in range(streams):
        piece_value = take(partial_value, s)
        if attentions:
            piece_value, _ = lax.optimization_barrier((piece_value, attentions[-1]))
        attentions.append(lax.psum(piece_value, "row"))
    finals = []
    for s in range(streams):
        mid_rows = take(image_split, s) + modifiers[:, 2] * attentions[s].astype(jnp.float32)
        normed = modulate(mid_rows, modifiers[:, 3], modifiers[:, 4]).astype(jnp.bfloat16)
        hidden_units = jax.nn.gelu(
            jnp.dot(normed.reshape(-1, model_width), up_weight, preferred_element_type=jnp.float32),
            approximate=True,
        ).astype(jnp.bfloat16)
        product = jnp.dot(hidden_units, down_weight, preferred_element_type=jnp.float32)
        product = product.reshape(prompts, rows_n * part, model_width).astype(jnp.bfloat16)
        if s + 1 < streams:
            product, attentions[s + 1] = lax.optimization_barrier((product, attentions[s + 1]))
        feed = lax.psum_scatter(product, "row", scatter_dimension=1, tiled=True).astype(jnp.float32)
        mid_own = lax.dynamic_index_in_dim(
            mid_rows.reshape(prompts, rows_n, part, model_width), row_idx, 1, keepdims=False
        )
        finals.append(mid_own + modifiers[:, 5] * feed)
    final_rows = jnp.concatenate(finals, axis=1)
    final_in = modulate(final_rows, modifiers[:, 8], modifiers[:, 9]).astype(jnp.bfloat16)
    own_velocity = jnp.dot(
        final_in.reshape(-1, model_width), final_weight, preferred_element_type=jnp.float32
    )
    own_velocity = own_velocity.reshape(1, prompts, own_rows, -1)
    half = lax.axis_index("cfg")
    width = own_velocity.shape[-1] // 2
    mine = lax.dynamic_slice_in_dim(own_velocity[0], half * width, width, 2)
    wanted = lax.dynamic_slice_in_dim(own_velocity[0], (1 - half) * width, width, 2)
    received = lax.ppermute(wanted, "cfg", [(0, 1), (1, 0)])
    conditional = jnp.where(half == 0, mine, received)
    unconditional = jnp.where(half == 0, received, mine)
    velocity = unconditional + guidance[0] * (conditional - unconditional)
    sigma_pair = lax.dynamic_slice_in_dim(sigmas, step_index[0], 2, 0)
    return (velocity, latents + (sigma_pair[1] - sigma_pair[0]) * velocity)


def solution(mesh):
    placed = (
        P("cfg", None, ("row", "col"), None),
        P("cfg", None, "row", None),
        P("cfg", None),
        P("cfg", None, None, None),
        P(),
        P(None, "row", None),
        P(None, "row", None),
        P("row", None, None),
        P(None, "row"),
        P("row", None),
        P(),
        P(None, ("row", "col"), "cfg"),
        P(),
        P(),
        P(),
    )
    return jax.shard_map(
        shards,
        mesh=mesh,
        in_specs=placed,
        out_specs=(P(None, ("row", "col"), "cfg"), P(None, ("row", "col"), "cfg")),
        check_vma=False,
    )
```
